256 devices in a mesh: ctx: 32 (over z_hi, x, y), head: 8 (over z_lo, core).
Axes of the slice: x: 4, y: 4, z: 8 (z_hi: 2, z_lo: 4; z = z_hi * 4 + z_lo), core: 2. Of those that a mesh axis runs over, the one named last changes fastest.
Arguments:
- queries: bfloat16 [12288, 4096], P('ctx', 'head'), may hold values from -200 to 200
- key_matrix: bfloat16 [12288, 1024], P('ctx', 'head'), may hold values from -6 to 6
- value_matrix: bfloat16 [12288, 1024], P('ctx', 'head'), may hold values from -6 to 6
- doc_ids: int32 [12288], P('ctx'), may hold values from 0 to 15, never falling along the last dimension, each value on 1 to 6528 neighbouring positions
- out_weight: bfloat16 [4096, 4096], P('head'), may hold values from -0.09375 to 0.09375
Outputs:
- projected: bfloat16 [12288, 4096], P(('ctx', 'head'))
The draws below stay inside these ranges and needn't reach their ends.
Inputs may be any that keep to these rules, and one draw needn't show every extreme that they name: `doc_ids`: document ids never fall along the tokens; each document has 1 to 6528 tokens and one has exactly 6528.
All inputs are finite; a program needn't handle non-finite values.
Results may differ from the reference program's by a relative error of at most 0.019.
Values may be sent and summed in bfloat16 or wider, within the bound.
No kernel may reach another device: no remote copies, remote signals or barrier semaphores. Data moves between devices by JAX's collectives and lax.ppermute only.
A program may use at most 256 MiB of HBM per device.

```python
import math
import jax
import jax.numpy as jnp
import numpy as np
from jax import lax

D = 4096
QUERY_HEADS = 32
KEY_VALUE_HEADS = 8
HEAD_WIDTH = 128
PACKED_TOKENS = 12288
MOST = 6528
DOCS = 16


def make_pair(key):
    base_key = jax.random.fold_in(key, 11)
    key_query, key_random_seeds = jax.random.split(base_key, 2)
    query_draw = jnp.clip(jax.random.normal(key_query, (PACKED_TOKENS, QUERY_HEADS * HEAD_WIDTH), jnp.float32), -6.0, 6.0)
    key_sample = jnp.clip(jax.random.normal(key_random_seeds, (PACKED_TOKENS, KEY_VALUE_HEADS * HEAD_WIDTH), jnp.float32), -6.0, 6.0)
    return (query_draw, key_sample)


def draw_queries(key, part):
    return make_pair(key)[0].astype(jnp.bfloat16)


def draw_key_matrix(key, part):
    return make_pair(key)[1].astype(jnp.bfloat16)


def level_of(rng, dims, cuts, least, high):
    gain, own = 1.0, jax.random.fold_in(rng, 6)
    for position, shards_of in cuts:
        draws = jnp.exp(jax.random.uniform(jax.random.fold_in(own, position), (shards_of,), jnp.float32, least / len(cuts), high / len(cuts)))
        gain = gain * jnp.repeat(draws, dims[position] // shards_of).reshape([-1 if axis == position else 1 for axis in range(len(dims))])
    return gain


def length_profile(count, total, bound, lean):
    portions = [(1 << 20) // math.isqrt(standing ** lean) + 1 for standing in range(2, count + 1)]
    spare, given = total - bound - (count - 1), [1] * (count - 1)
    while spare > 0:
        movable = [i for i in range(count - 1) if given[i] < bound]
        pool, remaining = sum([portions[i] for i in movable]), spare
        for i in movable:
            addition = min(bound - given[i], max(1, remaining * portions[i] // pool), spare)
            given[i] = given[i] + addition
            spare = spare - addition
    return np.array([bound] + given)


def uneven_parts(rng, number_of, total, most, lean):
    if number_of == 2:
        one = jax.random.randint(rng, (), max(1, total - most), min(most, total - 1) + 1)
        return jnp.stack([one, total - one])
    sizes = jnp.asarray(length_profile(number_of, total, most, lean), jnp.int32)
    twos = (number_of - 1) // 2
    source_of, sink = sizes[1:1 + 2 * twos:2], sizes[2:2 + 2 * twos:2]
    room = jnp.minimum(source_of - 1, most - sink)
    shifted = jax.random.randint(jax.random.fold_in(rng, 1), (twos,), 0, 1 << 20) % (room + 1)
    sizes = sizes.at[1:1 + 2 * twos:2].set(source_of - shifted).at[2:2 + 2 * twos:2].set(sink + shifted)
    return sizes[jax.random.permutation(jax.random.fold_in(rng, 2), number_of)]


def normal_values(stream_key, shape, spread, bound, pieces=(), kind=jnp.bfloat16):
    array = jax.random.normal(stream_key, shape, jnp.float32) * spread
    if len(pieces) > 0:
        array = level_of(stream_key, shape, pieces, -0.22, 0.18) * array
    return jnp.clip(array, min=-bound, max=bound).astype(kind)


def setup_inputs(seed: int = 0) -> dict:
    keys = jax.random.split(jax.random.key(seed), 6)
    return {
        "queries": draw_queries(jax.random.fold_in(keys[5], 71), 0),
        "key_matrix": draw_key_matrix(jax.random.fold_in(keys[5], 71), 0),
        "value_matrix": normal_values(keys[2], (PACKED_TOKENS, KEY_VALUE_HEADS * HEAD_WIDTH), 1.0, 6.0, ((0, 32), (1, 8))),
        "doc_ids": jnp.searchsorted(jnp.cumsum(uneven_parts(keys[3], DOCS, PACKED_TOKENS, MOST, 2)), jnp.arange(PACKED_TOKENS), side="right").astype(jnp.int32),
        "out_weight": normal_values(keys[4], (QUERY_HEADS * HEAD_WIDTH, D), (QUERY_HEADS * HEAD_WIDTH) ** -0.5, 0.09375, ((0, 8),)),
    }


def reference(queries, key_matrix, value_matrix, doc_ids, out_weight):
    queries_per_group = QUERY_HEADS // KEY_VALUE_HEADS
    query_heads = queries.reshape(PACKED_TOKENS, QUERY_HEADS, HEAD_WIDTH)
    key_head_split = key_matrix.reshape(PACKED_TOKENS, KEY_VALUE_HEADS, HEAD_WIDTH)
    value_head_split = value_matrix.reshape(PACKED_TOKENS, KEY_VALUE_HEADS, HEAD_WIDTH)
    positions = jnp.arange(PACKED_TOKENS, dtype=jnp.int32)
    allowed = (doc_ids[:, None] == doc_ids[None, :]) & (positions[:, None] >= positions[None, :])
    score_scale = HEAD_WIDTH ** -0.5

    def one_head(head_index):
        kv_index = head_index // queries_per_group
        query_head = lax.dynamic_index_in_dim(query_heads, head_index, 1, False)
        key_head = lax.dynamic_index_in_dim(key_head_split, kv_index, 1, False)
        value_head = lax.dynamic_index_in_dim(value_head_split, kv_index, 1, False)
        scores = jnp.dot(query_head, key_head.T, preferred_element_type=jnp.float32) * score_scale
        scores = jnp.where(allowed, scores, jnp.float32(-1e30))
        row_max = jnp.max(scores, axis=1)
        weights = jnp.where(allowed, jnp.exp(scores - row_max[:, None]), jnp.float32(0.0))
        denominator = jnp.sum(weights, axis=1)
        weighted = jnp.dot(weights.astype(jnp.bfloat16), value_head, preferred_element_type=jnp.float32)
        return (weighted / denominator[:, None]).astype(jnp.bfloat16)

    per_head = lax.map(one_head, jnp.arange(QUERY_HEADS, dtype=jnp.int32))
    attended = jnp.transpose(per_head, (1, 0, 2)).reshape(PACKED_TOKENS, QUERY_HEADS * HEAD_WIDTH)
    return jnp.dot(attended, out_weight, preferred_element_type=jnp.float32).astype(jnp.bfloat16)
```

```python
import functools
import math

import jax
import jax.numpy as jnp
import numpy as np
from jax import lax
from jax.experimental import pallas as pl
from jax.experimental.pallas import tpu as pltpu
from jax.sharding import Mesh, PartitionSpec as P

HEAD_WIDTH = 128
MOST = 6528
DOCS = 16
NEG = -1e30


def attn_kernel(steps, rows, heads, scale, sc_ref, q_ref, k_ref, v_ref, qs_ref, o_ref, m_sc, l_sc, acc_sc):
    j = pl.program_id(0)
    me = sc_ref[0]
    first = sc_ref[1]
    q_last_start = sc_ref[2]
    shard = me - (steps - 1) + j

    @pl.when(j == 0)
    def _init():
        m_sc[...] = jnp.full(m_sc.shape, NEG, jnp.float32)
        l_sc[...] = jnp.zeros(l_sc.shape, jnp.float32)
        acc_sc[...] = jnp.zeros(acc_sc.shape, jnp.float32)

    def block(masked):
        k = k_ref[...]
        v = v_ref[...]
        if masked:
            k_pos = shard * rows + lax.broadcasted_iota(jnp.int32, (rows, rows), 1)
            q_pos = me * rows + lax.broadcasted_iota(jnp.int32, (rows, rows), 0)
            allowed = (k_pos >= qs_ref[:, 0:1]) & (k_pos <= q_pos)
        for h in range(heads):
            qh = q_ref[:, h * HEAD_WIDTH:(h + 1) * HEAD_WIDTH]
            s = lax.dot_general(qh, k, (((1,), (1,)), ((), ())), preferred_element_type=jnp.float32)
            if masked:
                s = jnp.where(allowed, s, NEG)
            m_prev = m_sc[h]
            m_next = jnp.maximum(m_prev, jnp.max(s, axis=1, keepdims=True))
            p = jnp.exp((s - m_next[:, 0:1]) * scale)
            if masked:
                p = jnp.where(allowed, p, 0.0)
            alpha = jnp.exp((m_prev - m_next) * scale)
            l_sc[h] = alpha * l_sc[h] + jnp.sum(p, axis=1, keepdims=True)
            pv = jnp.dot(p.astype(jnp.bfloat16), v, preferred_element_type=jnp.float32)
            acc_sc[h] = alpha[:, 0:1] * acc_sc[h] + pv
            m_sc[h] = m_next

    live = shard >= first
    full = (shard < me) & (shard * rows >= q_last_start)

    @pl.when(live & full)
    def _full():
        block(False)

    @pl.when(live & jnp.logical_not(full))
    def _masked():
        block(True)

    @pl.when(j == steps - 1)
    def _finish():
        for h in range(heads):
            o_ref[:, h * HEAD_WIDTH:(h + 1) * HEAD_WIDTH] = (
                acc_sc[h] / l_sc[h][:, 0:1]
            ).astype(o_ref.dtype)


def attention(scalars, queries, kv, q_start, n_xy):
    rows, width = queries.shape
    heads = width // HEAD_WIDTH
    steps = -(-(MOST - 1) // rows) + 1
    scale = HEAD_WIDTH ** (-0.5)

    def shard_of(j, sc):
        return jnp.maximum(sc[0] - (steps - 1) + j, sc[1])

    def k_map(j, sc):
        s = shard_of(j, sc)
        return (s % n_xy, s // n_xy, 0, 0)

    def v_map(j, sc):
        s = shard_of(j, sc)
        return (s % n_xy, s // n_xy, 0, 1)

    kernel = functools.partial(attn_kernel, steps, rows, heads, scale)
    flops = 4 * steps * heads * rows * rows * HEAD_WIDTH
    return pl.pallas_call(
        kernel,
        out_shape=jax.ShapeDtypeStruct((rows, width), jnp.bfloat16),
        grid_spec=pltpu.PrefetchScalarGridSpec(
            num_scalar_prefetch=1,
            grid=(steps,),
            in_specs=[
                pl.BlockSpec((rows, width), lambda j, sc: (0, 0)),
                pl.BlockSpec((None, None, rows, HEAD_WIDTH), k_map),
                pl.BlockSpec((None, None, rows, HEAD_WIDTH), v_map),
                pl.BlockSpec((rows, 128), lambda j, sc: (0, 0)),
            ],
            out_specs=pl.BlockSpec((rows, width), lambda j, sc: (0, 0)),
            scratch_shapes=[
                pltpu.VMEM((heads, rows, 128), jnp.float32),
                pltpu.VMEM((heads, rows, 128), jnp.float32),
                pltpu.VMEM((heads, rows, HEAD_WIDTH), jnp.float32),
            ],
        ),
        compiler_params=pltpu.CompilerParams(dimension_semantics=("arbitrary",)),
        cost_estimate=pl.CostEstimate(
            flops=flops,
            transcendentals=steps * heads * rows * rows,
            bytes_accessed=steps * rows * 2 * HEAD_WIDTH * 2 + 2 * rows * width * 2,
        ),
    )(scalars, queries, kv, kv, q_start)


def per_device(n_xy, queries, key_matrix, value_matrix, doc_ids, out_weight):
    rows = queries.shape[0]
    me = lax.axis_index("zh") * n_xy + lax.axis_index("xy")

    hist = jnp.sum(
        (doc_ids[:, None] == jnp.arange(DOCS, dtype=jnp.int32)[None, :]).astype(jnp.float32), axis=0
    )
    counts = lax.psum(hist, ("zh", "xy"))
    below = (jnp.arange(DOCS, dtype=jnp.int32)[None, :] < doc_ids[:, None]).astype(jnp.float32)
    q_start = jnp.sum(below * counts[None, :], axis=1).astype(jnp.int32)
    first = jnp.maximum(q_start[0] // rows, 0)
    scalars = jnp.stack([me, first, q_start[rows - 1], jnp.int32(0)]).astype(jnp.int32)
    q_start_b = jnp.broadcast_to(q_start[:, None], (rows, 128))

    kv = jnp.concatenate([key_matrix, value_matrix], axis=1)
    kv = lax.all_gather(kv, "zh")
    kv = lax.all_gather(kv, "xy")

    attended = attention(scalars, queries, kv, q_start_b, n_xy)
    projected = jnp.dot(attended, out_weight, preferred_element_type=jnp.float32).astype(jnp.bfloat16)
    return lax.psum_scatter(projected, "head", scatter_dimension=0, tiled=True)


def solution(mesh):
    n_ctx = mesh.shape["ctx"]
    n_zh = 2
    n_xy = n_ctx // n_zh
    devices = np.asarray(mesh.devices).reshape(n_zh, n_xy, mesh.shape["head"])
    inner = Mesh(devices, ("zh", "xy", "head"))
    ctx = ("zh", "xy")
    placed = (P(ctx, "head"), P(ctx, "head"), P(ctx, "head"), P(ctx), P("head", None))
    return jax.shard_map(
        functools.partial(per_device, n_xy),
        mesh=inner,
        in_specs=placed,
        out_specs=P(("zh", "xy", "head"), None),
        check_vma=False,
    )
```

```python
import functools
import math

import jax
import jax.numpy as jnp
import numpy as np
from jax import lax
from jax.experimental import pallas as pl
from jax.experimental.pallas import tpu as pltpu
from jax.sharding import Mesh, PartitionSpec as P

HEAD_WIDTH = 128
MOST = 6528
DOCS = 16
NEG = -1e30


def attn_kernel(
    steps, rows, heads, scale, n_xy,
    sc_ref, q_ref, k1_ref, v1_ref, k2_ref, v2_ref, qs_ref, o_ref, m_sc, l_sc, acc_sc,
):
    j = pl.program_id(0)
    me = sc_ref[0]
    first = sc_ref[1]
    q_last_start = sc_ref[2]
    zh = sc_ref[3]
    shard = me - (steps - 1) + j

    @pl.when(j == 0)
    def _init():
        m_sc[...] = jnp.full(m_sc.shape, NEG, jnp.float32)
        l_sc[...] = jnp.zeros(l_sc.shape, jnp.float32)
        acc_sc[...] = jnp.zeros(acc_sc.shape, jnp.float32)

    def block(masked, k_ref, v_ref):
        k = k_ref[...]
        v = v_ref[...]
        if masked:
            k_pos = shard * rows + lax.broadcasted_iota(jnp.int32, (rows, rows), 1)
            q_pos = me * rows + lax.broadcasted_iota(jnp.int32, (rows, rows), 0)
            allowed = (k_pos >= qs_ref[:, 0:1]) & (k_pos <= q_pos)
        for h in range(heads):
            qh = q_ref[:, h * HEAD_WIDTH:(h + 1) * HEAD_WIDTH]
            s = lax.dot_general(qh, k, (((1,), (1,)), ((), ())), preferred_element_type=jnp.float32)
            if masked:
                s = jnp.where(allowed, s, NEG)
            m_prev = m_sc[h]
            m_next = jnp.maximum(m_prev, jnp.max(s, axis=1, keepdims=True))
            p = jnp.exp((s - m_next[:, 0:1]) * scale)
            if masked:
                p = jnp.where(allowed, p, 0.0)
            alpha = jnp.exp((m_prev - m_next) * scale)
            l_sc[h] = alpha * l_sc[h] + jnp.sum(p, axis=1, keepdims=True)
            pv = jnp.dot(p.astype(jnp.bfloat16), v, preferred_element_type=jnp.float32)
            acc_sc[h] = alpha[:, 0:1] * acc_sc[h] + pv
            m_sc[h] = m_next

    live = shard >= first
    full = (shard < me) & (shard * rows >= q_last_start)
    other = shard < zh * n_xy

    for masked in (False, True):
        kind = jnp.logical_not(full) if masked else full
        for use_other in (False, True):
            where_ = other if use_other else jnp.logical_not(other)
            refs = (k2_ref, v2_ref) if use_other else (k1_ref, v1_ref)
            pl.when(live & kind & where_)(functools.partial(block, masked, *refs))

    @pl.when(j == steps - 1)
    def _finish():
        for h in range(heads):
            o_ref[:, h * HEAD_WIDTH:(h + 1) * HEAD_WIDTH] = (
                acc_sc[h] / l_sc[h][:, 0:1]
            ).astype(o_ref.dtype)


def attention(scalars, queries, own, other, q_start, n_xy):
    rows, width = queries.shape
    heads = width // HEAD_WIDTH
    steps = -(-(MOST - 1) // rows) + 1
    scale = HEAD_WIDTH ** (-0.5)

    def shard_of(j, sc):
        return jnp.maximum(sc[0] - (steps - 1) + j, sc[1])

    def own_index(j, sc):
        base = sc[3] * n_xy
        low = jnp.maximum(sc[1] - base, 0)
        return jnp.minimum(jnp.maximum(shard_of(j, sc) - base, low), n_xy - 1)

    def other_index(j, sc):
        return jnp.where(sc[3] == 1, jnp.minimum(shard_of(j, sc), n_xy - 1), 0)

    kernel = functools.partial(attn_kernel, steps, rows, heads, scale, n_xy)
    flops = 4 * steps * heads * rows * rows * HEAD_WIDTH
    return pl.pallas_call(
        kernel,
        out_shape=jax.ShapeDtypeStruct((rows, width), jnp.bfloat16),
        grid_spec=pltpu.PrefetchScalarGridSpec(
            num_scalar_prefetch=1,
            grid=(steps,),
            in_specs=[
                pl.BlockSpec((rows, width), lambda j, sc: (0, 0)),
                pl.BlockSpec((None, rows, HEAD_WIDTH), lambda j, sc: (own_index(j, sc), 0, 0)),
                pl.BlockSpec((None, rows, HEAD_WIDTH), lambda j, sc: (own_index(j, sc), 0, 1)),
                pl.BlockSpec((None, rows, HEAD_WIDTH), lambda j, sc: (other_index(j, sc), 0, 0)),
                pl.BlockSpec((None, rows, HEAD_WIDTH), lambda j, sc: (other_index(j, sc), 0, 1)),
                pl.BlockSpec((rows, 128), lambda j, sc: (0, 0)),
            ],
            out_specs=pl.BlockSpec((rows, width), lambda j, sc: (0, 0)),
            scratch_shapes=[
                pltpu.VMEM((heads, rows, 128), jnp.float32),
                pltpu.VMEM((heads, rows, 128), jnp.float32),
                pltpu.VMEM((heads, rows, HEAD_WIDTH), jnp.float32),
            ],
        ),
        compiler_params=pltpu.CompilerParams(dimension_semantics=("arbitrary",)),
        cost_estimate=pl.CostEstimate(
            flops=flops,
            transcendentals=steps * heads * rows * rows,
            bytes_accessed=steps * rows * 2 * HEAD_WIDTH * 2 + 2 * rows * width * 2,
        ),
    )(scalars, queries, own, own, other, other, q_start)


def per_device(n_xy, queries, key_matrix, value_matrix, doc_ids, out_weight):
    rows = queries.shape[0]
    zh = lax.axis_index("zh")
    me = zh * n_xy + lax.axis_index("xy")

    kv = jnp.concatenate([key_matrix, value_matrix], axis=1)
    lanes = kv.shape[1]
    tile = 8
    ids = jnp.full((tile * lanes,), -1.0, jnp.float32).at[:rows].set(doc_ids.astype(jnp.float32))
    block = jnp.concatenate([kv, ids.reshape(tile, lanes).astype(kv.dtype)], axis=0)

    own = lax.all_gather(block, "xy")
    partner = lax.ppermute(block, "zh", perm=[(0, 1), (1, 0)])
    other = lax.all_gather(partner, "xy")

    id_rows = jnp.concatenate([own[:, rows:, :], other[:, rows:, :]], axis=0).astype(jnp.float32)
    docs = jnp.arange(DOCS, dtype=jnp.float32)
    counts = jnp.sum((id_rows[..., None] == docs).astype(jnp.float32), axis=(0, 1, 2))
    below = (jnp.arange(DOCS, dtype=jnp.int32)[None, :] < doc_ids[:, None]).astype(jnp.float32)
    q_start = jnp.sum(below * counts[None, :], axis=1).astype(jnp.int32)
    first = jnp.maximum(q_start[0] // rows, 0)
    scalars = jnp.stack([me, first, q_start[rows - 1], zh]).astype(jnp.int32)
    q_start_b = jnp.broadcast_to(q_start[:, None], (rows, 128))

    attended = attention(scalars, queries, own, other, q_start_b, n_xy)
    projected = jnp.dot(attended, out_weight, preferred_element_type=jnp.float32).astype(jnp.bfloat16)
    return lax.psum_scatter(projected, "head", scatter_dimension=0, tiled=True)


def solution(mesh):
    n_ctx = mesh.shape["ctx"]
    n_zh = 2
    n_xy = n_ctx // n_zh
    devices = np.asarray(mesh.devices).reshape(n_zh, n_xy, mesh.shape["head"])
    inner = Mesh(devices, ("zh", "xy", "head"))
    ctx = ("zh", "xy")
    placed = (P(ctx, "head"), P(ctx, "head"), P(ctx, "head"), P(ctx), P("head", None))
    return jax.shard_map(
        functools.partial(per_device, n_xy),
        mesh=inner,
        in_specs=placed,
        out_specs=P(("zh", "xy", "head"), None),
        check_vma=False,
    )
```

```python
import functools

import jax
import jax.numpy as jnp
import numpy as np
from jax import lax
from jax.experimental import pallas as pl
from jax.experimental.pallas import tpu as pltpu
from jax.sharding import Mesh, PartitionSpec as P

HEAD_WIDTH = 128
LANES = 128
MOST = 6528
DOCS = 16
NEG = -1e30
CHUNKS = 2


def attn_kernel(steps, shard_rows, heads, scale, sc_ref, q_ref, k_ref, v_ref, qs_ref, qp_ref, o_ref, m_sc, l_sc, acc_sc):
    j = pl.program_id(0)
    me = sc_ref[0]
    first = sc_ref[1]
    q_last_start = sc_ref[2]
    shard = me - (steps - 1) + j
    rows = q_ref.shape[0]

    @pl.when(j == 0)
    def _init():
        m_sc[...] = jnp.full(m_sc.shape, NEG, jnp.float32)
        l_sc[...] = jnp.zeros(l_sc.shape, jnp.float32)
        acc_sc[...] = jnp.zeros(acc_sc.shape, jnp.float32)

    def block(masked):
        k = k_ref[...]
        v = v_ref[...]
        if masked:
            k_pos = shard * shard_rows + lax.broadcasted_iota(jnp.int32, (rows, shard_rows), 1)
            allowed = (k_pos >= qs_ref[:, 0:1]) & (k_pos <= qp_ref[:, 0:1])
        for h in range(heads):
            qh = q_ref[:, h * HEAD_WIDTH:(h + 1) * HEAD_WIDTH]
            s = lax.dot_general(qh, k, (((1,), (1,)), ((), ())), preferred_element_type=jnp.float32)
            if masked:
                s = jnp.where(allowed, s, NEG)
            m_prev = m_sc[h]
            m_next = jnp.maximum(m_prev, jnp.max(s, axis=1, keepdims=True))
            p = jnp.exp((s - m_next[:, 0:1]) * scale)
            if masked:
                p = jnp.where(allowed, p, 0.0)
            alpha = jnp.exp((m_prev - m_next) * scale)
            part = p[:, 0:LANES]
            for c in range(1, shard_rows // LANES):
                part = part + p[:, c * LANES:(c + 1) * LANES]
            l_sc[h] = alpha * l_sc[h] + part
            pv = jnp.dot(p.astype(jnp.bfloat16), v, preferred_element_type=jnp.float32)
            acc_sc[h] = alpha[:, 0:1] * acc_sc[h] + pv
            m_sc[h] = m_next

    live = shard >= first
    full = (shard < me) & (shard * shard_rows >= q_last_start)

    @pl.when(live & full)
    def _full():
        block(False)

    @pl.when(live & jnp.logical_not(full))
    def _masked():
        block(True)

    @pl.when(j == steps - 1)
    def _finish():
        for h in range(heads):
            denominator = jnp.sum(l_sc[h], axis=1, keepdims=True)
            o_ref[:, h * HEAD_WIDTH:(h + 1) * HEAD_WIDTH] = (acc_sc[h] / denominator).astype(o_ref.dtype)


def attention(scalars, queries, kv, q_start, q_pos, n_xy, shard_rows):
    rows, width = queries.shape
    heads = width // HEAD_WIDTH
    steps = -(-(MOST - 1) // shard_rows) + 1
    scale = HEAD_WIDTH ** (-0.5)

    def index(j, sc, half):
        s = jnp.maximum(sc[0] - (steps - 1) + j, sc[1])
        slot = jnp.where(s // n_xy == sc[3], 0, 1)
        return (s % n_xy, slot, 0, half)

    kernel = functools.partial(attn_kernel, steps, shard_rows, heads, scale)
    return pl.pallas_call(
        kernel,
        out_shape=jax.ShapeDtypeStruct((rows, width), jnp.bfloat16),
        grid_spec=pltpu.PrefetchScalarGridSpec(
            num_scalar_prefetch=1,
            grid=(steps,),
            in_specs=[
                pl.BlockSpec((rows, width), lambda j, sc: (0, 0)),
                pl.BlockSpec((None, None, shard_rows, HEAD_WIDTH), lambda j, sc: index(j, sc, 0)),
                pl.BlockSpec((None, None, shard_rows, HEAD_WIDTH), lambda j, sc: index(j, sc, 1)),
                pl.BlockSpec((rows, LANES), lambda j, sc: (0, 0)),
                pl.BlockSpec((rows, LANES), lambda j, sc: (0, 0)),
            ],
            out_specs=pl.BlockSpec((rows, width), lambda j, sc: (0, 0)),
            scratch_shapes=[
                pltpu.VMEM((heads, rows, LANES), jnp.float32),
                pltpu.VMEM((heads, rows, LANES), jnp.float32),
                pltpu.VMEM((heads, rows, HEAD_WIDTH), jnp.float32),
            ],
        ),
        compiler_params=pltpu.CompilerParams(dimension_semantics=("arbitrary",)),
        cost_estimate=pl.CostEstimate(
            flops=4 * steps * heads * rows * shard_rows * HEAD_WIDTH,
            transcendentals=steps * heads * rows * shard_rows,
            bytes_accessed=steps * shard_rows * 2 * HEAD_WIDTH * 2 + 2 * rows * width * 2,
        ),
    )(scalars, queries, kv, kv, q_start, q_pos)


def per_device(n_xy, n_head, queries, key_matrix, value_matrix, doc_ids, out_weight):
    rows = queries.shape[0]
    zh = lax.axis_index("zh")
    me = zh * n_xy + lax.axis_index("xy")

    kv = jnp.concatenate([key_matrix, value_matrix], axis=1)
    lanes = kv.shape[1]
    tile = 8
    ids = jnp.full((tile * lanes,), -1.0, jnp.float32).at[:rows].set(doc_ids.astype(jnp.float32))
    block = jnp.concatenate([kv, ids.reshape(tile, lanes).astype(kv.dtype)], axis=0)

    partner = lax.ppermute(block, "zh", perm=[(0, 1), (1, 0)])
    pair = jnp.stack([block, partner])
    gathered = lax.all_gather(pair, "xy")

    id_rows = gathered[:, :, rows:, :].astype(jnp.float32)
    docs = jnp.arange(DOCS, dtype=jnp.float32)
    counts = jnp.sum((id_rows[..., None] == docs).astype(jnp.float32), axis=(0, 1, 2, 3))
    below = (jnp.arange(DOCS, dtype=jnp.int32)[None, :] < doc_ids[:, None]).astype(jnp.float32)
    q_start = jnp.sum(below * counts[None, :], axis=1).astype(jnp.int32)
    q_pos = me * rows + jnp.arange(rows, dtype=jnp.int32)

    per_head = rows // n_head
    piece = per_head // CHUNKS

    def chunk_of(x, c):
        x = x.reshape((n_head, CHUNKS, piece) + x.shape[1:])[:, c]
        return x.reshape((n_head * piece,) + x.shape[2:])

    outs = []
    for c in range(CHUNKS):
        qs_c = chunk_of(q_start, c)
        qp_c = chunk_of(q_pos, c)
        first = jnp.maximum(qs_c[0] // rows, 0)
        scalars = jnp.stack([me, first, qs_c[-1], zh]).astype(jnp.int32)
        attended = attention(
            scalars,
            chunk_of(queries, c),
            gathered,
            jnp.broadcast_to(qs_c[:, None], (qs_c.shape[0], LANES)),
            jnp.broadcast_to(qp_c[:, None], (qp_c.shape[0], LANES)),
            n_xy,
            rows,
        )
        projected = jnp.dot(attended, out_weight, preferred_element_type=jnp.float32).astype(jnp.bfloat16)
        outs.append(lax.psum_scatter(projected, "head", scatter_dimension=0, tiled=True))
    return jnp.concatenate(outs, axis=0)


def solution(mesh):
    n_ctx = mesh.shape["ctx"]
    n_head = mesh.shape["head"]
    n_zh = 2
    n_xy = n_ctx // n_zh
    devices = np.asarray(mesh.devices).reshape(n_zh, n_xy, n_head)
    inner = Mesh(devices, ("zh", "xy", "head"))
    ctx = ("zh", "xy")
    placed = (P(ctx, "head"), P(ctx, "head"), P(ctx, "head"), P(ctx), P("head", None))
    return jax.shard_map(
        functools.partial(per_device, n_xy, n_head),
        mesh=inner,
        in_specs=placed,
        out_specs=P(("zh", "xy", "head"), None),
        check_vma=False,
    )
```

```python
import functools

import jax
import jax.numpy as jnp
import numpy as np
from jax import lax
from jax.experimental import pallas as pl
from jax.experimental.pallas import tpu as pltpu
from jax.sharding import Mesh, PartitionSpec as P

HEAD_WIDTH = 128
LANES = 128
MOST = 6528
DOCS = 16
NEG = -1e30
CHUNKS = 2
SUB = 64


def attn_kernel(steps, shard_rows, heads, scale, sc_ref, q_ref, k_ref, v_ref, qs_ref, qp_ref, o_ref, m_sc, l_sc, acc_sc):
    j = pl.program_id(0)
    me = sc_ref[0]
    first = sc_ref[1]
    q_last_start = sc_ref[2]
    shard = me - (steps - 1) + j
    rows = q_ref.shape[0]

    @pl.when(j == 0)
    def _init():
        m_sc[...] = jnp.full(m_sc.shape, NEG, jnp.float32)
        l_sc[...] = jnp.zeros(l_sc.shape, jnp.float32)
        acc_sc[...] = jnp.zeros(acc_sc.shape, jnp.float32)

    def block(masked):
        def sub_block(h, i, carry):
            r = pl.ds(pl.multiple_of(i * SUB, SUB), SUB)
            qh = q_ref[r, h * HEAD_WIDTH:(h + 1) * HEAD_WIDTH]
            s = lax.dot_general(qh, k_ref[...], (((1,), (1,)), ((), ())), preferred_element_type=jnp.float32)
            if masked:
                k_pos = shard * shard_rows + lax.broadcasted_iota(jnp.int32, (SUB, shard_rows), 1)
                allowed = (k_pos >= qs_ref[r, 0:1]) & (k_pos <= qp_ref[r, 0:1])
                s = jnp.where(allowed, s, NEG)
            m_prev = m_sc[h, r, :]
            m_next = jnp.maximum(m_prev, jnp.max(s, axis=1, keepdims=True))
            p = jnp.exp((s - m_next[:, 0:1]) * scale)
            if masked:
                p = jnp.where(allowed, p, 0.0)
            alpha = jnp.exp((m_prev - m_next) * scale)
            part = p[:, 0:LANES]
            for c in range(1, shard_rows // LANES):
                part = part + p[:, c * LANES:(c + 1) * LANES]
            l_sc[h, r, :] = alpha * l_sc[h, r, :] + part
            pv = jnp.dot(p.astype(jnp.bfloat16), v_ref[...], preferred_element_type=jnp.float32)
            acc_sc[h, r, :] = alpha[:, 0:1] * acc_sc[h, r, :] + pv
            m_sc[h, r, :] = m_next
            return carry

        for h in range(heads):
            lax.fori_loop(0, rows // SUB, functools.partial(sub_block, h), 0)

    live = shard >= first
    full = (shard < me) & (shard * shard_rows >= q_last_start)

    @pl.when(live & full)
    def _full():
        block(False)

    @pl.when(live & jnp.logical_not(full))
    def _masked():
        block(True)

    @pl.when(j == steps - 1)
    def _finish():
        for h in range(heads):
            denominator = jnp.sum(l_sc[h], axis=1, keepdims=True)
            o_ref[:, h * HEAD_WIDTH:(h + 1) * HEAD_WIDTH] = (acc_sc[h] / denominator).astype(o_ref.dtype)


def attention(scalars, queries, kv, q_start, q_pos, n_xy, shard_rows):
    rows, width = queries.shape
    heads = width // HEAD_WIDTH
    steps = -(-(MOST - 1) // shard_rows) + 1
    scale = HEAD_WIDTH ** (-0.5)

    def index(j, sc, half):
        s = jnp.maximum(sc[0] - (steps - 1) + j, sc[1])
        slot = jnp.where(s // n_xy == sc[3], 0, 1)
        return (s % n_xy, slot, 0, half)

    kernel = functools.partial(attn_kernel, steps, shard_rows, heads, scale)
    return pl.pallas_call(
        kernel,
        out_shape=jax.ShapeDtypeStruct((rows, width), jnp.bfloat16),
        grid_spec=pltpu.PrefetchScalarGridSpec(
            num_scalar_prefetch=1,
            grid=(steps,),
            in_specs=[
                pl.BlockSpec((rows, width), lambda j, sc: (0, 0)),
                pl.BlockSpec((None, None, shard_rows, HEAD_WIDTH), lambda j, sc: index(j, sc, 0)),
                pl.BlockSpec((None, None, shard_rows, HEAD_WIDTH), lambda j, sc: index(j, sc, 1)),
                pl.BlockSpec((rows, LANES), lambda j, sc: (0, 0)),
                pl.BlockSpec((rows, LANES), lambda j, sc: (0, 0)),
            ],
            out_specs=pl.BlockSpec((rows, width), lambda j, sc: (0, 0)),
            scratch_shapes=[
                pltpu.VMEM((heads, rows, LANES), jnp.float32),
                pltpu.VMEM((heads, rows, LANES), jnp.float32),
                pltpu.VMEM((heads, rows, HEAD_WIDTH), jnp.float32),
            ],
        ),
        compiler_params=pltpu.CompilerParams(dimension_semantics=("arbitrary",)),
        cost_estimate=pl.CostEstimate(
            flops=4 * steps * heads * rows * shard_rows * HEAD_WIDTH,
            transcendentals=steps * heads * rows * shard_rows,
            bytes_accessed=steps * shard_rows * 2 * HEAD_WIDTH * 2 + 2 * rows * width * 2,
        ),
    )(scalars, queries, kv, kv, q_start, q_pos)


def per_device(n_xy, n_head, queries, key_matrix, value_matrix, doc_ids, out_weight):
    rows = queries.shape[0]
    zh = lax.axis_index("zh")
    me = zh * n_xy + lax.axis_index("xy")

    kv = jnp.concatenate([key_matrix, value_matrix], axis=1)
    lanes = kv.shape[1]
    tile = 8
    ids = jnp.full((tile * lanes,), -1.0, jnp.float32).at[:rows].set(doc_ids.astype(jnp.float32))
    block = jnp.concatenate([kv, ids.reshape(tile, lanes).astype(kv.dtype)], axis=0)

    partner = lax.ppermute(block, "zh", perm=[(0, 1), (1, 0)])
    pair = jnp.stack([block, partner])
    gathered = lax.all_gather(pair, "xy")

    id_rows = gathered[:, :, rows:, :].astype(jnp.float32)
    docs = jnp.arange(DOCS, dtype=jnp.float32)
    counts = jnp.sum((id_rows[..., None] == docs).astype(jnp.float32), axis=(0, 1, 2, 3))
    below = (jnp.arange(DOCS, dtype=jnp.int32)[None, :] < doc_ids[:, None]).astype(jnp.float32)
    q_start = jnp.sum(below * counts[None, :], axis=1).astype(jnp.int32)
    q_pos = me * rows + jnp.arange(rows, dtype=jnp.int32)

    per_head = rows // n_head
    piece = per_head // CHUNKS

    def chunk_of(x, c):
        x = x.reshape((n_head, CHUNKS, piece) + x.shape[1:])[:, c]
        return x.reshape((n_head * piece,) + x.shape[2:])

    outs = []
    for c in range(CHUNKS):
        qs_c = chunk_of(q_start, c)
        qp_c = chunk_of(q_pos, c)
        first = jnp.maximum(qs_c[0] // rows, 0)
        scalars = jnp.stack([me, first, qs_c[-1], zh]).astype(jnp.int32)
        attended = attention(
            scalars,
            chunk_of(queries, c),
            gathered,
            jnp.broadcast_to(qs_c[:, None], (qs_c.shape[0], LANES)),
            jnp.broadcast_to(qp_c[:, None], (qp_c.shape[0], LANES)),
            n_xy,
            rows,
        )
        projected = jnp.dot(attended, out_weight, preferred_element_type=jnp.float32).astype(jnp.bfloat16)
        outs.append(lax.psum_scatter(projected, "head", scatter_dimension=0, tiled=True))
    return jnp.concatenate(outs, axis=0)


def solution(mesh):
    n_ctx = mesh.shape["ctx"]
    n_head = mesh.shape["head"]
    n_zh = 2
    n_xy = n_ctx // n_zh
    devices = np.asarray(mesh.devices).reshape(n_zh, n_xy, n_head)
    inner = Mesh(devices, ("zh", "xy", "head"))
    ctx = ("zh", "xy")
    placed = (P(ctx, "head"), P(ctx, "head"), P(ctx, "head"), P(ctx), P("head", None))
    return jax.shard_map(
        functools.partial(per_device, n_xy, n_head),
        mesh=inner,
        in_specs=placed,
        out_specs=P(("zh", "xy", "head"), None),
        check_vma=False,
    )
```

```python
import functools

import jax
import jax.numpy as jnp
import numpy as np
from jax import lax
from jax.experimental import pallas as pl
from jax.experimental.pallas import tpu as pltpu
from jax.sharding import Mesh, PartitionSpec as P

HEAD_WIDTH = 128
LANES = 128
MOST = 6528
DOCS = 16
NEG = -1e30
CHUNKS = 2


def attn_kernel(steps, shard_rows, heads, scale, sc_ref, q_ref, k_ref, v_ref, qs_ref, qp_ref, o_ref, m_sc, l_sc, acc_sc):
    j = pl.program_id(0)
    me = sc_ref[0]
    first = sc_ref[1]
    q_last_start = sc_ref[2]
    shard = me - (steps - 1) + j
    rows = q_ref.shape[0]

    @pl.when(j == 0)
    def _init():
        m_sc[...] = jnp.full(m_sc.shape, NEG, jnp.float32)
        l_sc[...] = jnp.zeros(l_sc.shape, jnp.float32)
        acc_sc[...] = jnp.zeros(acc_sc.shape, jnp.float32)

    def block(masked):
        cols = shard_rows // LANES
        if masked:
            lane = lax.broadcasted_iota(jnp.int32, (rows, LANES), 1)
            allowed = []
            for c in range(cols):
                k_pos = shard * shard_rows + c * LANES + lane
                allowed.append((k_pos >= qs_ref[:, 0:1]) & (k_pos <= qp_ref[:, 0:1]))
        for h in range(heads):
            qh = q_ref[:, h * HEAD_WIDTH:(h + 1) * HEAD_WIDTH]
            s = []
            for c in range(cols):
                s_c = jnp.dot(qh, k_ref[c * LANES:(c + 1) * LANES, :], preferred_element_type=jnp.float32)
                if masked:
                    s_c = jnp.where(allowed[c], s_c, NEG)
                s.append(s_c)
            top = s[0]
            for c in range(1, cols):
                top = jnp.maximum(top, s[c])
            m_prev = m_sc[h]
            m_next = jnp.maximum(m_prev, jnp.max(top, axis=1, keepdims=True))
            m_b = m_next[:, 0:1]
            part = None
            pv = None
            for c in range(cols):
                p = jnp.exp((s[c] - m_b) * scale)
                if masked:
                    p = jnp.where(allowed[c], p, 0.0)
                part = p if part is None else part + p
                term = jnp.dot(
                    p.astype(jnp.bfloat16), v_ref[c * LANES:(c + 1) * LANES, :], preferred_element_type=jnp.float32
                )
                pv = term if pv is None else pv + term
            alpha = jnp.exp((m_prev - m_next) * scale)
            l_sc[h] = alpha * l_sc[h] + part
            acc_sc[h] = alpha[:, 0:1] * acc_sc[h] + pv
            m_sc[h] = m_next

    live = shard >= first
    full = (shard < me) & (shard * shard_rows >= q_last_start)

    @pl.when(live & full)
    def _full():
        block(False)

    @pl.when(live & jnp.logical_not(full))
    def _masked():
        block(True)

    @pl.when(j == steps - 1)
    def _finish():
        for h in range(heads):
            denominator = jnp.sum(l_sc[h], axis=1, keepdims=True)
            o_ref[:, h * HEAD_WIDTH:(h + 1) * HEAD_WIDTH] = (acc_sc[h] / denominator).astype(o_ref.dtype)


def attention(scalars, queries, kv, q_start, q_pos, n_xy, shard_rows):
    rows, width = queries.shape
    heads = width // HEAD_WIDTH
    steps = -(-(MOST - 1) // shard_rows) + 1
    scale = HEAD_WIDTH ** (-0.5)

    def index(j, sc, half):
        s = jnp.maximum(sc[0] - (steps - 1) + j, sc[1])
        slot = jnp.where(s // n_xy == sc[3], 0, 1)
        return (s % n_xy, slot, 0, half)

    kernel = functools.partial(attn_kernel, steps, shard_rows, heads, scale)
    return pl.pallas_call(
        kernel,
        out_shape=jax.ShapeDtypeStruct((rows, width), jnp.bfloat16),
        grid_spec=pltpu.PrefetchScalarGridSpec(
            num_scalar_prefetch=1,
            grid=(steps,),
            in_specs=[
                pl.BlockSpec((rows, width), lambda j, sc: (0, 0)),
                pl.BlockSpec((None, None, shard_rows, HEAD_WIDTH), lambda j, sc: index(j, sc, 0)),
                pl.BlockSpec((None, None, shard_rows, HEAD_WIDTH), lambda j, sc: index(j, sc, 1)),
                pl.BlockSpec((rows, LANES), lambda j, sc: (0, 0)),
                pl.BlockSpec((rows, LANES), lambda j, sc: (0, 0)),
            ],
            out_specs=pl.BlockSpec((rows, width), lambda j, sc: (0, 0)),
            scratch_shapes=[
                pltpu.VMEM((heads, rows, LANES), jnp.float32),
                pltpu.VMEM((heads, rows, LANES), jnp.float32),
                pltpu.VMEM((heads, rows, HEAD_WIDTH), jnp.float32),
            ],
        ),
        compiler_params=pltpu.CompilerParams(dimension_semantics=("arbitrary",)),
        cost_estimate=pl.CostEstimate(
            flops=4 * steps * heads * rows * shard_rows * HEAD_WIDTH,
            transcendentals=steps * heads * rows * shard_rows,
            bytes_accessed=steps * shard_rows * 2 * HEAD_WIDTH * 2 + 2 * rows * width * 2,
        ),
    )(scalars, queries, kv, kv, q_start, q_pos)


def per_device(n_xy, n_head, queries, key_matrix, value_matrix, doc_ids, out_weight):
    rows = queries.shape[0]
    zh = lax.axis_index("zh")
    me = zh * n_xy + lax.axis_index("xy")

    width = key_matrix.shape[1]
    k_t = key_matrix.T.reshape(width, rows // LANES, LANES).transpose(1, 0, 2).reshape(rows, width)
    kv = jnp.concatenate([k_t, value_matrix], axis=1)
    lanes = kv.shape[1]
    tile = 8
    ids = jnp.full((tile * lanes,), -1.0, jnp.float32).at[:rows].set(doc_ids.astype(jnp.float32))
    block = jnp.concatenate([kv, ids.reshape(tile, lanes).astype(kv.dtype)], axis=0)

    partner = lax.ppermute(block, "zh", perm=[(0, 1), (1, 0)])
    pair = jnp.stack([block, partner])
    gathered = lax.all_gather(pair, "xy")

    id_rows = gathered[:, :, rows:, :].astype(jnp.float32)
    docs = jnp.arange(DOCS, dtype=jnp.float32)
    counts = jnp.sum((id_rows[..., None] == docs).astype(jnp.float32), axis=(0, 1, 2, 3))
    below = (jnp.arange(DOCS, dtype=jnp.int32)[None, :] < doc_ids[:, None]).astype(jnp.float32)
    q_start = jnp.sum(below * counts[None, :], axis=1).astype(jnp.int32)
    q_pos = me * rows + jnp.arange(rows, dtype=jnp.int32)

    per_head = rows // n_head
    piece = per_head // CHUNKS

    def chunk_of(x, c):
        x = x.reshape((n_head, CHUNKS, piece) + x.shape[1:])[:, c]
        return x.reshape((n_head * piece,) + x.shape[2:])

    outs = []
    for c in range(CHUNKS):
        qs_c = chunk_of(q_start, c)
        qp_c = chunk_of(q_pos, c)
        first = jnp.maximum(qs_c[0] // rows, 0)
        scalars = jnp.stack([me, first, qs_c[-1], zh]).astype(jnp.int32)
        attended = attention(
            scalars,
            chunk_of(queries, c),
            gathered,
            jnp.broadcast_to(qs_c[:, None], (qs_c.shape[0], LANES)),
            jnp.broadcast_to(qp_c[:, None], (qp_c.shape[0], LANES)),
            n_xy,
            rows,
        )
        projected = jnp.dot(attended, out_weight, preferred_element_type=jnp.float32).astype(jnp.bfloat16)
        outs.append(lax.psum_scatter(projected, "head", scatter_dimension=0, tiled=True))
    return jnp.concatenate(outs, axis=0)


def solution(mesh):
    n_ctx = mesh.shape["ctx"]
    n_head = mesh.shape["head"]
    n_zh = 2
    n_xy = n_ctx // n_zh
    devices = np.asarray(mesh.devices).reshape(n_zh, n_xy, n_head)
    inner = Mesh(devices, ("zh", "xy", "head"))
    ctx = ("zh", "xy")
    placed = (P(ctx, "head"), P(ctx, "head"), P(ctx, "head"), P(ctx), P("head", None))
    return jax.shard_map(
        functools.partial(per_device, n_xy, n_head),
        mesh=inner,
        in_specs=placed,
        out_specs=P(("zh", "xy", "head"), None),
        check_vma=False,
    )
```

```python
import functools

import jax
import jax.numpy as jnp
import numpy as np
from jax import lax
from jax.experimental import pallas as pl
from jax.experimental.pallas import tpu as pltpu
from jax.sharding import Mesh, PartitionSpec as P

HEAD_WIDTH = 128
LANES = 128
MOST = 6528
DOCS = 16
NEG = -1e30
CHUNKS = 2


def attn_kernel(
    steps, shard_rows, heads, scale, sc_ref, q_ref, k_ref, v_ref, qs_ref, qp_ref, after_ref, o_ref, m_sc, l_sc, acc_sc
):
    j = pl.program_id(0)
    me = sc_ref[0]
    first = sc_ref[1]
    q_last_start = sc_ref[2]
    shard = me - (steps - 1) + j
    rows = q_ref.shape[0]

    @pl.when(j == 0)
    def _init():
        m_sc[...] = jnp.full(m_sc.shape, NEG, jnp.float32)
        l_sc[...] = jnp.zeros(l_sc.shape, jnp.float32)
        acc_sc[...] = jnp.zeros(acc_sc.shape, jnp.float32)

    def block(masked):
        cols = shard_rows // LANES
        if masked:
            lane = lax.broadcasted_iota(jnp.int32, (rows, LANES), 1)
            allowed = []
            for c in range(cols):
                k_pos = shard * shard_rows + c * LANES + lane
                allowed.append((k_pos >= qs_ref[:, 0:1]) & (k_pos <= qp_ref[:, 0:1]))
        for h in range(heads):
            qh = q_ref[:, h * HEAD_WIDTH:(h + 1) * HEAD_WIDTH]
            s = []
            for c in range(cols):
                s_c = jnp.dot(qh, k_ref[c * LANES:(c + 1) * LANES, :], preferred_element_type=jnp.float32)
                if masked:
                    s_c = jnp.where(allowed[c], s_c, NEG)
                s.append(s_c)
            top = s[0]
            for c in range(1, cols):
                top = jnp.maximum(top, s[c])
            m_prev = m_sc[h]
            m_next = jnp.maximum(m_prev, jnp.max(top, axis=1, keepdims=True))
            m_b = m_next[:, 0:1]
            part = None
            pv = None
            for c in range(cols):
                p = jnp.exp((s[c] - m_b) * scale)
                if masked:
                    p = jnp.where(allowed[c], p, 0.0)
                part = p if part is None else part + p
                term = jnp.dot(
                    p.astype(jnp.bfloat16), v_ref[c * LANES:(c + 1) * LANES, :], preferred_element_type=jnp.float32
                )
                pv = term if pv is None else pv + term
            alpha = jnp.exp((m_prev - m_next) * scale)
            l_sc[h] = alpha * l_sc[h] + part
            acc_sc[h] = alpha[:, 0:1] * acc_sc[h] + pv
            m_sc[h] = m_next

    live = shard >= first
    full = (shard < me) & (shard * shard_rows >= q_last_start)

    @pl.when(live & full)
    def _full():
        block(False)

    @pl.when(live & jnp.logical_not(full))
    def _masked():
        block(True)

    @pl.when(j == steps - 1)
    def _finish():
        for h in range(heads):
            denominator = jnp.sum(l_sc[h], axis=1, keepdims=True)
            o_ref[:, h * HEAD_WIDTH:(h + 1) * HEAD_WIDTH] = (acc_sc[h] / denominator).astype(o_ref.dtype)


def attention(scalars, queries, kv, q_start, q_pos, after, n_xy, shard_rows):
    rows, width = queries.shape
    heads = width // HEAD_WIDTH
    steps = -(-(MOST - 1) // shard_rows) + 1
    scale = HEAD_WIDTH ** (-0.5)

    def index(j, sc, half):
        s = jnp.maximum(sc[0] - (steps - 1) + j, sc[1])
        slot = jnp.where(s // n_xy == sc[3], 0, 1)
        return (s % n_xy, slot, 0, half)

    kernel = functools.partial(attn_kernel, steps, shard_rows, heads, scale)
    return pl.pallas_call(
        kernel,
        out_shape=jax.ShapeDtypeStruct((rows, width), jnp.bfloat16),
        grid_spec=pltpu.PrefetchScalarGridSpec(
            num_scalar_prefetch=1,
            grid=(steps,),
            in_specs=[
                pl.BlockSpec((rows, width), lambda j, sc: (0, 0)),
                pl.BlockSpec((None, None, shard_rows, HEAD_WIDTH), lambda j, sc: index(j, sc, 0)),
                pl.BlockSpec((None, None, shard_rows, HEAD_WIDTH), lambda j, sc: index(j, sc, 1)),
                pl.BlockSpec((rows, LANES), lambda j, sc: (0, 0)),
                pl.BlockSpec((rows, LANES), lambda j, sc: (0, 0)),
                pl.BlockSpec(memory_space=pl.ANY),
            ],
            out_specs=pl.BlockSpec((rows, width), lambda j, sc: (0, 0)),
            scratch_shapes=[
                pltpu.VMEM((heads, rows, LANES), jnp.float32),
                pltpu.VMEM((heads, rows, LANES), jnp.float32),
                pltpu.VMEM((heads, rows, HEAD_WIDTH), jnp.float32),
            ],
        ),
        compiler_params=pltpu.CompilerParams(dimension_semantics=("arbitrary",)),
        cost_estimate=pl.CostEstimate(
            flops=4 * steps * heads * rows * shard_rows * HEAD_WIDTH,
            transcendentals=steps * heads * rows * shard_rows,
            bytes_accessed=steps * shard_rows * 2 * HEAD_WIDTH * 2 + 2 * rows * width * 2,
        ),
    )(scalars, queries, kv, kv, q_start, q_pos, after)


def per_device(n_xy, n_head, queries, key_matrix, value_matrix, doc_ids, out_weight):
    rows = queries.shape[0]
    zh = lax.axis_index("zh")
    me = zh * n_xy + lax.axis_index("xy")

    width = key_matrix.shape[1]
    k_t = key_matrix.T.reshape(width, rows // LANES, LANES).transpose(1, 0, 2).reshape(rows, width)
    kv = jnp.concatenate([k_t, value_matrix], axis=1)
    lanes = kv.shape[1]
    tile = 8
    ids = jnp.full((tile * lanes,), -1.0, jnp.float32).at[:rows].set(doc_ids.astype(jnp.float32))
    block = jnp.concatenate([kv, ids.reshape(tile, lanes).astype(kv.dtype)], axis=0)

    partner = lax.ppermute(block, "zh", perm=[(0, 1), (1, 0)])
    pair = jnp.stack([block, partner])
    gathered = lax.all_gather(pair, "xy")

    id_rows = gathered[:, :, rows:, :].astype(jnp.float32)
    docs = jnp.arange(DOCS, dtype=jnp.float32)
    counts = jnp.sum((id_rows[..., None] == docs).astype(jnp.float32), axis=(0, 1, 2, 3))
    below = (jnp.arange(DOCS, dtype=jnp.int32)[None, :] < doc_ids[:, None]).astype(jnp.float32)
    q_start = jnp.sum(below * counts[None, :], axis=1).astype(jnp.int32)
    q_pos = me * rows + jnp.arange(rows, dtype=jnp.int32)

    per_head = rows // n_head
    piece = per_head // CHUNKS

    def chunk_of(x, c):
        x = x.reshape((n_head, CHUNKS, piece) + x.shape[1:])[:, c]
        return x.reshape((n_head * piece,) + x.shape[2:])

    outs = []
    after = jnp.zeros((8, LANES), jnp.bfloat16)
    for c in range(CHUNKS):
        qs_c = chunk_of(q_start, c)
        qp_c = chunk_of(q_pos, c)
        first = jnp.maximum(qs_c[0] // rows, 0)
        scalars = jnp.stack([me, first, qs_c[-1], zh]).astype(jnp.int32)
        attended = attention(
            scalars,
            chunk_of(queries, c),
            gathered,
            jnp.broadcast_to(qs_c[:, None], (qs_c.shape[0], LANES)),
            jnp.broadcast_to(qp_c[:, None], (qp_c.shape[0], LANES)),
            after,
            n_xy,
            rows,
        )
        after = attended
        projected = jnp.dot(attended, out_weight, preferred_element_type=jnp.float32).astype(jnp.bfloat16)
        if c < CHUNKS - 1:
            outs.append(lax.psum_scatter(projected, "head", scatter_dimension=0, tiled=True))
        else:
            parts = projected.reshape((n_head, piece) + projected.shape[1:])
            parts = lax.all_to_all(parts, "head", 0, 0)
            outs.append(jnp.sum(parts.astype(jnp.float32), axis=0).astype(jnp.bfloat16))
    return jnp.concatenate(outs, axis=0)


def solution(mesh):
    n_ctx = mesh.shape["ctx"]
    n_head = mesh.shape["head"]
    n_zh = 2
    n_xy = n_ctx // n_zh
    devices = np.asarray(mesh.devices).reshape(n_zh, n_xy, n_head)
    inner = Mesh(devices, ("zh", "xy", "head"))
    ctx = ("zh", "xy")
    placed = (P(ctx, "head"), P(ctx, "head"), P(ctx, "head"), P(ctx), P("head", None))
    return jax.shard_map(
        functools.partial(per_device, n_xy, n_head),
        mesh=inner,
        in_specs=placed,
        out_specs=P(("zh", "xy", "head"), None),
        check_vma=False,
    )
```

```python
import functools

import jax
import jax.numpy as jnp
import numpy as np
from jax import lax
from jax.experimental import pallas as pl
from jax.experimental.pallas import tpu as pltpu
from jax.sharding import Mesh, PartitionSpec as P

HEAD_WIDTH = 128
LANES = 128
MOST = 6528
DOCS = 16
NEG = -1e30
CHUNKS = 2


def attn_kernel(
    steps, shard_rows, heads, scale, sc_ref, q_ref, k_ref, v_ref, qs_ref, qp_ref, after_ref, o_ref, m_sc, l_sc, acc_sc
):
    j = pl.program_id(0)
    me = sc_ref[0]
    first = sc_ref[1]
    q_last_start = sc_ref[2]
    shard = me - (steps - 1) + j
    rows = q_ref.shape[0]

    @pl.when(j == 0)
    def _init():
        m_sc[...] = jnp.full(m_sc.shape, NEG, jnp.float32)
        l_sc[...] = jnp.zeros(l_sc.shape, jnp.float32)
        acc_sc[...] = jnp.zeros(acc_sc.shape, jnp.float32)

    def block(masked):
        cols = shard_rows // LANES
        if masked:
            lane = lax.broadcasted_iota(jnp.int32, (rows, LANES), 1)
            allowed = []
            for c in range(cols):
                k_pos = shard * shard_rows + c * LANES + lane
                allowed.append((k_pos >= qs_ref[:, 0:1]) & (k_pos <= qp_ref[:, 0:1]))
        for h in range(heads):
            qh = q_ref[:, h * HEAD_WIDTH:(h + 1) * HEAD_WIDTH]
            s = []
            for c in range(cols):
                s_c = jnp.dot(qh, k_ref[c * LANES:(c + 1) * LANES, :], preferred_element_type=jnp.float32)
                if masked:
                    s_c = jnp.where(allowed[c], s_c, NEG)
                s.append(s_c)
            top = s[0]
            for c in range(1, cols):
                top = jnp.maximum(top, s[c])
            m_prev = m_sc[h]
            m_next = jnp.maximum(m_prev, jnp.max(top, axis=1, keepdims=True))
            m_b = m_next[:, 0:1]
            part = None
            pv = None
            for c in range(cols):
                p = jnp.exp((s[c] - m_b) * scale)
                if masked:
                    p = jnp.where(allowed[c], p, 0.0)
                part = p if part is None else part + p
                term = jnp.dot(
                    p.astype(jnp.bfloat16), v_ref[c * LANES:(c + 1) * LANES, :], preferred_element_type=jnp.float32
                )
                pv = term if pv is None else pv + term
            alpha = jnp.exp((m_prev - m_next) * scale)
            l_sc[h] = alpha * l_sc[h] + part
            acc_sc[h] = alpha[:, 0:1] * acc_sc[h] + pv
            m_sc[h] = m_next

    live = shard >= first
    full = (shard < me) & (shard * shard_rows >= q_last_start)

    @pl.when(live & full)
    def _full():
        block(False)

    @pl.when(live & jnp.logical_not(full))
    def _masked():
        block(True)

    @pl.when(j == steps - 1)
    def _finish():
        for h in range(heads):
            denominator = jnp.sum(l_sc[h], axis=1, keepdims=True)
            o_ref[:, h * HEAD_WIDTH:(h + 1) * HEAD_WIDTH] = (acc_sc[h] / denominator).astype(o_ref.dtype)


def attention(scalars, queries, kv, q_start, q_pos, after, n_xy, shard_rows):
    rows, width = queries.shape
    heads = width // HEAD_WIDTH
    steps = -(-(MOST - 1) // shard_rows) + 1
    scale = HEAD_WIDTH ** (-0.5)

    def index(j, sc, half):
        s = jnp.maximum(sc[0] - (steps - 1) + j, sc[1])
        slot = jnp.where(s // n_xy == sc[3], 0, 1)
        return (s % n_xy, slot, 0, half)

    kernel = functools.partial(attn_kernel, steps, shard_rows, heads, scale)
    return pl.pallas_call(
        kernel,
        out_shape=jax.ShapeDtypeStruct((rows, width), jnp.bfloat16),
        grid_spec=pltpu.PrefetchScalarGridSpec(
            num_scalar_prefetch=1,
            grid=(steps,),
            in_specs=[
                pl.BlockSpec((rows, width), lambda j, sc: (0, 0)),
                pl.BlockSpec((None, None, shard_rows, HEAD_WIDTH), lambda j, sc: index(j, sc, 0)),
                pl.BlockSpec((None, None, shard_rows, HEAD_WIDTH), lambda j, sc: index(j, sc, 1)),
                pl.BlockSpec((rows, LANES), lambda j, sc: (0, 0)),
                pl.BlockSpec((rows, LANES), lambda j, sc: (0, 0)),
                pl.BlockSpec(memory_space=pl.ANY),
            ],
            out_specs=pl.BlockSpec((rows, width), lambda j, sc: (0, 0)),
            scratch_shapes=[
                pltpu.VMEM((heads, rows, LANES), jnp.float32),
                pltpu.VMEM((heads, rows, LANES), jnp.float32),
                pltpu.VMEM((heads, rows, HEAD_WIDTH), jnp.float32),
            ],
        ),
        compiler_params=pltpu.CompilerParams(dimension_semantics=("arbitrary",)),
        cost_estimate=pl.CostEstimate(
            flops=4 * steps * heads * rows * shard_rows * HEAD_WIDTH,
            transcendentals=steps * heads * rows * shard_rows,
            bytes_accessed=steps * shard_rows * 2 * HEAD_WIDTH * 2 + 2 * rows * width * 2,
        ),
    )(scalars, queries, kv, kv, q_start, q_pos, after)


def per_device(n_xy, n_head, queries, key_matrix, value_matrix, doc_ids, out_weight):
    rows = queries.shape[0]
    zh = lax.axis_index("zh")
    me = zh * n_xy + lax.axis_index("xy")

    width = key_matrix.shape[1]
    k_t = key_matrix.T.reshape(width, rows // LANES, LANES).transpose(1, 0, 2).reshape(rows, width)
    kv = jnp.concatenate([k_t, value_matrix], axis=1)
    lanes = kv.shape[1]
    tile = 8
    ids = jnp.full((tile * lanes,), -1.0, jnp.float32).at[:rows].set(doc_ids.astype(jnp.float32))
    block = jnp.concatenate([kv, ids.reshape(tile, lanes).astype(kv.dtype)], axis=0)

    partner = lax.ppermute(block, "zh", perm=[(0, 1), (1, 0)])
    pair = jnp.stack([block, partner])
    gathered = lax.all_gather(pair, "xy")

    id_rows = gathered[:, :, rows:, :].astype(jnp.float32)
    docs = jnp.arange(DOCS, dtype=jnp.float32)
    counts = jnp.sum((id_rows[..., None] == docs).astype(jnp.float32), axis=(0, 1, 2, 3))
    below = (jnp.arange(DOCS, dtype=jnp.int32)[None, :] < doc_ids[:, None]).astype(jnp.float32)
    q_start = jnp.sum(below * counts[None, :], axis=1).astype(jnp.int32)
    q_pos = me * rows + jnp.arange(rows, dtype=jnp.int32)

    per_head = rows // n_head
    piece = per_head // CHUNKS

    def chunk_of(x, c):
        x = x.reshape((n_head, CHUNKS, piece) + x.shape[1:])[:, c]
        return x.reshape((n_head * piece,) + x.shape[2:])

    outs = []
    after = jnp.zeros((8, LANES), jnp.bfloat16)
    for c in range(CHUNKS):
        qs_c = chunk_of(q_start, c)
        qp_c = chunk_of(q_pos, c)
        first = jnp.maximum(qs_c[0] // rows, 0)
        scalars = jnp.stack([me, first, qs_c[-1], zh]).astype(jnp.int32)
        attended = attention(
            scalars,
            chunk_of(queries, c),
            gathered,
            jnp.broadcast_to(qs_c[:, None], (qs_c.shape[0], LANES)),
            jnp.broadcast_to(qp_c[:, None], (qp_c.shape[0], LANES)),
            after,
            n_xy,
            rows,
        )
        projected = jnp.dot(attended, out_weight, preferred_element_type=jnp.float32).astype(jnp.bfloat16)
        after = projected
        if c < CHUNKS - 1:
            outs.append(lax.psum_scatter(projected, "head", scatter_dimension=0, tiled=True))
        else:
            me_head = lax.axis_index("head")
            held = projected.reshape((n_head, piece) + projected.shape[1:]).astype(jnp.float32)
            bit = 1
            while bit < n_head:
                mine = (me_head // bit) % 2
                held = held.reshape((-1, 2) + held.shape[1:])
                keep = lax.dynamic_index_in_dim(held, mine, axis=1, keepdims=False)
                send = lax.dynamic_index_in_dim(held, 1 - mine, axis=1, keepdims=False)
                pairs = [(i, i ^ bit) for i in range(n_head)]
                got = lax.ppermute(send.astype(jnp.bfloat16), "head", perm=pairs)
                held = keep + got.astype(jnp.float32)
                bit *= 2
            outs.append(held[0].astype(jnp.bfloat16))
    return jnp.concatenate(outs, axis=0)


def solution(mesh):
    n_ctx = mesh.shape["ctx"]
    n_head = mesh.shape["head"]
    n_zh = 2
    n_xy = n_ctx // n_zh
    devices = np.asarray(mesh.devices).reshape(n_zh, n_xy, n_head)
    inner = Mesh(devices, ("zh", "xy", "head"))
    ctx = ("zh", "xy")
    placed = (P(ctx, "head"), P(ctx, "head"), P(ctx, "head"), P(ctx), P("head", None))
    return jax.shard_map(
        functools.partial(per_device, n_xy, n_head),
        mesh=inner,
        in_specs=placed,
        out_specs=P(("zh", "xy", "head"), None),
        check_vma=False,
    )
```

```python
import functools

import jax
import jax.numpy as jnp
import numpy as np
from jax import lax
from jax.experimental import pallas as pl
from jax.experimental.pallas import tpu as pltpu
from jax.sharding import Mesh, PartitionSpec as P

HEAD_WIDTH = 128
LANES = 128
MOST = 6528
DOCS = 16
NEG = -1e30
CHUNKS = 2


def attn_kernel(
    steps, shard_rows, heads, scale, sc_ref, q_ref, k_ref, v_ref, qs_ref, qp_ref, after_ref, o_ref, m_sc, l_sc, acc_sc
):
    j = pl.program_id(0)
    me = sc_ref[0]
    first = sc_ref[1]
    q_last_start = sc_ref[2]
    shard = me - (steps - 1) + j
    rows = q_ref.shape[0]

    @pl.when(j == 0)
    def _init():
        m_sc[...] = jnp.full(m_sc.shape, NEG, jnp.float32)
        l_sc[...] = jnp.zeros(l_sc.shape, jnp.float32)
        acc_sc[...] = jnp.zeros(acc_sc.shape, jnp.float32)

    def block(masked):
        cols = shard_rows // LANES
        if masked:
            lane = lax.broadcasted_iota(jnp.int32, (rows, LANES), 1)
            allowed = []
            for c in range(cols):
                k_pos = shard * shard_rows + c * LANES + lane
                allowed.append((k_pos >= qs_ref[:, 0:1]) & (k_pos <= qp_ref[:, 0:1]))
        for h in range(heads):
            qh = q_ref[:, h * HEAD_WIDTH:(h + 1) * HEAD_WIDTH]
            s = []
            for c in range(cols):
                s_c = jnp.dot(qh, k_ref[c * LANES:(c + 1) * LANES, :], preferred_element_type=jnp.float32)
                if masked:
                    s_c = jnp.where(allowed[c], s_c, NEG)
                s.append(s_c)
            top = s[0]
            for c in range(1, cols):
                top = jnp.maximum(top, s[c])
            m_prev = m_sc[h]
            m_next = jnp.maximum(m_prev, jnp.max(top, axis=1, keepdims=True))
            m_b = m_next[:, 0:1]
            part = None
            pv = None
            for c in range(cols):
                p = jnp.exp((s[c] - m_b) * scale)
                if masked:
                    p = jnp.where(allowed[c], p, 0.0)
                part = p if part is None else part + p
                term = jnp.dot(
                    p.astype(jnp.bfloat16), v_ref[c * LANES:(c + 1) * LANES, :], preferred_element_type=jnp.float32
                )
                pv = term if pv is None else pv + term
            alpha = jnp.exp((m_prev - m_next) * scale)
            l_sc[h] = alpha * l_sc[h] + part
            acc_sc[h] = alpha[:, 0:1] * acc_sc[h] + pv
            m_sc[h] = m_next

    live = shard >= first
    full = (shard < me) & (shard * shard_rows >= q_last_start)

    @pl.when(live & full)
    def _full():
        block(False)

    @pl.when(live & jnp.logical_not(full))
    def _masked():
        block(True)

    @pl.when(j == steps - 1)
    def _finish():
        for h in range(heads):
            denominator = jnp.sum(l_sc[h], axis=1, keepdims=True)
            o_ref[:, h * HEAD_WIDTH:(h + 1) * HEAD_WIDTH] = (acc_sc[h] / denominator).astype(o_ref.dtype)


def attention(scalars, queries, kv, q_start, q_pos, after, n_xy, shard_rows):
    rows, width = queries.shape
    heads = width // HEAD_WIDTH
    steps = -(-(MOST - 1) // shard_rows) + 1
    scale = HEAD_WIDTH ** (-0.5)

    def index(j, sc, half):
        s = jnp.maximum(sc[0] - (steps - 1) + j, sc[1])
        slot = jnp.where(s // n_xy == sc[3], 0, 1)
        return (s % n_xy, slot, 0, half)

    kernel = functools.partial(attn_kernel, steps, shard_rows, heads, scale)
    return pl.pallas_call(
        kernel,
        out_shape=jax.ShapeDtypeStruct((rows, width), jnp.bfloat16),
        grid_spec=pltpu.PrefetchScalarGridSpec(
            num_scalar_prefetch=1,
            grid=(steps,),
            in_specs=[
                pl.BlockSpec((rows, width), lambda j, sc: (0, 0)),
                pl.BlockSpec((None, None, shard_rows, HEAD_WIDTH), lambda j, sc: index(j, sc, 0)),
                pl.BlockSpec((None, None, shard_rows, HEAD_WIDTH), lambda j, sc: index(j, sc, 1)),
                pl.BlockSpec((rows, LANES), lambda j, sc: (0, 0)),
                pl.BlockSpec((rows, LANES), lambda j, sc: (0, 0)),
                pl.BlockSpec(memory_space=pl.ANY),
            ],
            out_specs=pl.BlockSpec((rows, width), lambda j, sc: (0, 0)),
            scratch_shapes=[
                pltpu.VMEM((heads, rows, LANES), jnp.float32),
                pltpu.VMEM((heads, rows, LANES), jnp.float32),
                pltpu.VMEM((heads, rows, HEAD_WIDTH), jnp.float32),
            ],
        ),
        compiler_params=pltpu.CompilerParams(dimension_semantics=("arbitrary",)),
        cost_estimate=pl.CostEstimate(
            flops=4 * steps * heads * rows * shard_rows * HEAD_WIDTH,
            transcendentals=steps * heads * rows * shard_rows,
            bytes_accessed=steps * shard_rows * 2 * HEAD_WIDTH * 2 + 2 * rows * width * 2,
        ),
    )(scalars, queries, kv, kv, q_start, q_pos, after)


def sum_over_heads(projected, n_head, piece):
    me_head = lax.axis_index("head")
    held = projected.reshape((n_head // 2, 2, piece) + projected.shape[1:]).astype(jnp.float32)
    core = me_head % 2
    keep = lax.dynamic_index_in_dim(held, core, axis=1, keepdims=False)
    send = lax.dynamic_index_in_dim(held, 1 - core, axis=1, keepdims=False)
    got = lax.ppermute(send.astype(jnp.bfloat16), "head", perm=[(i, i ^ 1) for i in range(n_head)])
    held = keep + got.astype(jnp.float32)
    chip = me_head // 2
    total = lax.dynamic_index_in_dim(held, chip, axis=0, keepdims=False)
    for k in range(1, n_head // 2):
        send = lax.dynamic_index_in_dim(held, chip ^ k, axis=0, keepdims=False)
        got = lax.ppermute(send.astype(jnp.bfloat16), "head", perm=[(i, i ^ (2 * k)) for i in range(n_head)])
        total = total + got.astype(jnp.float32)
    return total.astype(jnp.bfloat16)


def per_device(n_xy, n_head, queries, key_matrix, value_matrix, doc_ids, out_weight):
    rows = queries.shape[0]
    zh = lax.axis_index("zh")
    me = zh * n_xy + lax.axis_index("xy")

    width = key_matrix.shape[1]
    k_t = key_matrix.T.reshape(width, rows // LANES, LANES).transpose(1, 0, 2).reshape(rows, width)
    kv = jnp.concatenate([k_t, value_matrix], axis=1)
    lanes = kv.shape[1]
    tile = 8
    ids = jnp.full((tile * lanes,), -1.0, jnp.float32).at[:rows].set(doc_ids.astype(jnp.float32))
    block = jnp.concatenate([kv, ids.reshape(tile, lanes).astype(kv.dtype)], axis=0)

    partner = lax.ppermute(block, "zh", perm=[(0, 1), (1, 0)])
    pair = jnp.stack([block, partner])
    gathered = lax.all_gather(pair, "xy")

    id_rows = gathered[:, :, rows:, :].astype(jnp.float32)
    docs = jnp.arange(DOCS, dtype=jnp.float32)
    counts = jnp.sum((id_rows[..., None] == docs).astype(jnp.float32), axis=(0, 1, 2, 3))
    below = (jnp.arange(DOCS, dtype=jnp.int32)[None, :] < doc_ids[:, None]).astype(jnp.float32)
    q_start = jnp.sum(below * counts[None, :], axis=1).astype(jnp.int32)
    q_pos = me * rows + jnp.arange(rows, dtype=jnp.int32)

    per_head = rows // n_head
    piece = per_head // CHUNKS

    def chunk_of(x, c):
        x = x.reshape((n_head, CHUNKS, piece) + x.shape[1:])[:, c]
        return x.reshape((n_head * piece,) + x.shape[2:])

    outs = []
    after = jnp.zeros((8, LANES), jnp.bfloat16)
    for c in range(CHUNKS):
        qs_c = chunk_of(q_start, c)
        qp_c = chunk_of(q_pos, c)
        first = jnp.maximum(qs_c[0] // rows, 0)
        scalars = jnp.stack([me, first, qs_c[-1], zh]).astype(jnp.int32)
        attended = attention(
            scalars,
            chunk_of(queries, c),
            gathered,
            jnp.broadcast_to(qs_c[:, None], (qs_c.shape[0], LANES)),
            jnp.broadcast_to(qp_c[:, None], (qp_c.shape[0], LANES)),
            after,
            n_xy,
            rows,
        )
        projected = jnp.dot(attended, out_weight, preferred_element_type=jnp.float32).astype(jnp.bfloat16)
        after = projected
        outs.append(sum_over_heads(projected, n_head, piece))
    return jnp.concatenate(outs, axis=0)


def solution(mesh):
    n_ctx = mesh.shape["ctx"]
    n_head = mesh.shape["head"]
    n_zh = 2
    n_xy = n_ctx // n_zh
    devices = np.asarray(mesh.devices).reshape(n_zh, n_xy, n_head)
    inner = Mesh(devices, ("zh", "xy", "head"))
    ctx = ("zh", "xy")
    placed = (P(ctx, "head"), P(ctx, "head"), P(ctx, "head"), P(ctx), P("head", None))
    return jax.shard_map(
        functools.partial(per_device, n_xy, n_head),
        mesh=inner,
        in_specs=placed,
        out_specs=P(("zh", "xy", "head"), None),
        check_vma=False,
    )
```

```python
import functools

import jax
import jax.numpy as jnp
import numpy as np
from jax import lax
from jax.experimental import pallas as pl
from jax.experimental.pallas import tpu as pltpu
from jax.sharding import Mesh, PartitionSpec as P

HEAD_WIDTH = 128
LANES = 128
MOST = 6528
DOCS = 16
NEG = -1e30
CHUNKS = 2


def attn_kernel(
    steps, shard_rows, heads, scale, sc_ref, q_ref, k_ref, v_ref, qs_ref, qp_ref, after_ref, o_ref, m_sc, l_sc, acc_sc
):
    j = pl.program_id(0)
    me = sc_ref[0]
    first = sc_ref[1]
    q_last_start = sc_ref[2]
    shard = me - (steps - 1) + j
    rows = q_ref.shape[0]

    @pl.when(j == 0)
    def _init():
        m_sc[...] = jnp.full(m_sc.shape, NEG, jnp.float32)
        l_sc[...] = jnp.zeros(l_sc.shape, jnp.float32)
        acc_sc[...] = jnp.zeros(acc_sc.shape, jnp.float32)

    def block(masked):
        cols = shard_rows // LANES
        if masked:
            lane = lax.broadcasted_iota(jnp.int32, (rows, LANES), 1)
            allowed = []
            for c in range(cols):
                k_pos = shard * shard_rows + c * LANES + lane
                allowed.append((k_pos >= qs_ref[:, 0:1]) & (k_pos <= qp_ref[:, 0:1]))
        for h in range(heads):
            qh = q_ref[:, h * HEAD_WIDTH:(h + 1) * HEAD_WIDTH]
            s = []
            for c in range(cols):
                s_c = jnp.dot(qh, k_ref[c * LANES:(c + 1) * LANES, :], preferred_element_type=jnp.float32)
                if masked:
                    s_c = jnp.where(allowed[c], s_c, NEG)
                s.append(s_c)
            top = s[0]
            for c in range(1, cols):
                top = jnp.maximum(top, s[c])
            m_prev = m_sc[h]
            m_next = jnp.maximum(m_prev, jnp.max(top, axis=1, keepdims=True))
            m_b = m_next[:, 0:1]
            part = None
            pv = None
            for c in range(cols):
                p = jnp.exp((s[c] - m_b) * scale)
                if masked:
                    p = jnp.where(allowed[c], p, 0.0)
                part = p if part is None else part + p
                term = jnp.dot(
                    p.astype(jnp.bfloat16), v_ref[c * LANES:(c + 1) * LANES, :], preferred_element_type=jnp.float32
                )
                pv = term if pv is None else pv + term
            alpha = jnp.exp((m_prev - m_next) * scale)
            l_sc[h] = alpha * l_sc[h] + part
            acc_sc[h] = alpha[:, 0:1] * acc_sc[h] + pv
            m_sc[h] = m_next

    live = shard >= first
    full = (shard < me) & (shard * shard_rows >= q_last_start)

    @pl.when(live & full)
    def _full():
        block(False)

    @pl.when(live & jnp.logical_not(full))
    def _masked():
        block(True)

    @pl.when(j == steps - 1)
    def _finish():
        for h in range(heads):
            denominator = jnp.sum(l_sc[h], axis=1, keepdims=True)
            o_ref[:, h * HEAD_WIDTH:(h + 1) * HEAD_WIDTH] = (acc_sc[h] / denominator).astype(o_ref.dtype)


def attention(scalars, queries, kv, q_start, q_pos, after, n_xy, shard_rows):
    rows, width = queries.shape
    heads = width // HEAD_WIDTH
    steps = -(-(MOST - 1) // shard_rows) + 1
    scale = HEAD_WIDTH ** (-0.5)

    def index(j, sc, half):
        s = jnp.maximum(sc[0] - (steps - 1) + j, sc[1])
        slot = jnp.where(s // n_xy == sc[3], 0, 1)
        return (s % n_xy, slot, 0, half)

    kernel = functools.partial(attn_kernel, steps, shard_rows, heads, scale)
    return pl.pallas_call(
        kernel,
        out_shape=jax.ShapeDtypeStruct((rows, width), jnp.bfloat16),
        grid_spec=pltpu.PrefetchScalarGridSpec(
            num_scalar_prefetch=1,
            grid=(steps,),
            in_specs=[
                pl.BlockSpec((rows, width), lambda j, sc: (0, 0)),
                pl.BlockSpec((None, None, shard_rows, HEAD_WIDTH), lambda j, sc: index(j, sc, 0)),
                pl.BlockSpec((None, None, shard_rows, HEAD_WIDTH), lambda j, sc: index(j, sc, 1)),
                pl.BlockSpec((rows, LANES), lambda j, sc: (0, 0)),
                pl.BlockSpec((rows, LANES), lambda j, sc: (0, 0)),
                pl.BlockSpec(memory_space=pl.ANY),
            ],
            out_specs=pl.BlockSpec((rows, width), lambda j, sc: (0, 0)),
            scratch_shapes=[
                pltpu.VMEM((heads, rows, LANES), jnp.float32),
                pltpu.VMEM((heads, rows, LANES), jnp.float32),
                pltpu.VMEM((heads, rows, HEAD_WIDTH), jnp.float32),
            ],
        ),
        compiler_params=pltpu.CompilerParams(dimension_semantics=("arbitrary",)),
        cost_estimate=pl.CostEstimate(
            flops=4 * steps * heads * rows * shard_rows * HEAD_WIDTH,
            transcendentals=steps * heads * rows * shard_rows,
            bytes_accessed=steps * shard_rows * 2 * HEAD_WIDTH * 2 + 2 * rows * width * 2,
        ),
    )(scalars, queries, kv, kv, q_start, q_pos, after)


def core_step(projected, n_head, piece):
    me_head = lax.axis_index("head")
    held = projected.reshape((n_head // 2, 2, piece) + projected.shape[1:]).astype(jnp.float32)
    core = me_head % 2
    keep = lax.dynamic_index_in_dim(held, core, axis=1, keepdims=False)
    send = lax.dynamic_index_in_dim(held, 1 - core, axis=1, keepdims=False)
    got = lax.ppermute(send.astype(jnp.bfloat16), "head", perm=[(i, i ^ 1) for i in range(n_head)])
    return keep + got.astype(jnp.float32)


def chip_step(held, n_head):
    chip = lax.axis_index("head") // 2
    total = lax.dynamic_index_in_dim(held, chip, axis=1, keepdims=False)
    for k in range(1, n_head // 2):
        send = lax.dynamic_index_in_dim(held, chip ^ k, axis=1, keepdims=False)
        got = lax.ppermute(send.astype(jnp.bfloat16), "head", perm=[(i, i ^ (2 * k)) for i in range(n_head)])
        total = total + got.astype(jnp.float32)
    return total.astype(jnp.bfloat16)


def per_device(n_xy, n_head, queries, key_matrix, value_matrix, doc_ids, out_weight):
    rows = queries.shape[0]
    zh = lax.axis_index("zh")
    me = zh * n_xy + lax.axis_index("xy")

    width = key_matrix.shape[1]
    k_t = key_matrix.T.reshape(width, rows // LANES, LANES).transpose(1, 0, 2).reshape(rows, width)
    kv = jnp.concatenate([k_t, value_matrix], axis=1)
    lanes = kv.shape[1]
    tile = 8
    ids = jnp.full((tile * lanes,), -1.0, jnp.float32).at[:rows].set(doc_ids.astype(jnp.float32))
    block = jnp.concatenate([kv, ids.reshape(tile, lanes).astype(kv.dtype)], axis=0)

    partner = lax.ppermute(block, "zh", perm=[(0, 1), (1, 0)])
    pair = jnp.stack([block, partner])
    gathered = lax.all_gather(pair, "xy")

    id_rows = gathered[:, :, rows:, :].astype(jnp.float32)
    docs = jnp.arange(DOCS, dtype=jnp.float32)
    counts = jnp.sum((id_rows[..., None] == docs).astype(jnp.float32), axis=(0, 1, 2, 3))
    below = (jnp.arange(DOCS, dtype=jnp.int32)[None, :] < doc_ids[:, None]).astype(jnp.float32)
    q_start = jnp.sum(below * counts[None, :], axis=1).astype(jnp.int32)
    q_pos = me * rows + jnp.arange(rows, dtype=jnp.int32)

    per_head = rows // n_head
    piece = per_head // CHUNKS

    def chunk_of(x, c):
        x = x.reshape((n_head, CHUNKS, piece) + x.shape[1:])[:, c]
        return x.reshape((n_head * piece,) + x.shape[2:])

    outs = []
    after = jnp.zeros((8, LANES), jnp.bfloat16)
    for c in range(CHUNKS):
        qs_c = chunk_of(q_start, c)
        qp_c = chunk_of(q_pos, c)
        first = jnp.maximum(qs_c[0] // rows, 0)
        scalars = jnp.stack([me, first, qs_c[-1], zh]).astype(jnp.int32)
        attended = attention(
            scalars,
            chunk_of(queries, c),
            gathered,
            jnp.broadcast_to(qs_c[:, None], (qs_c.shape[0], LANES)),
            jnp.broadcast_to(qp_c[:, None], (qp_c.shape[0], LANES)),
            after,
            n_xy,
            rows,
        )
        projected = jnp.dot(attended, out_weight, preferred_element_type=jnp.float32).astype(jnp.bfloat16)
        held = core_step(projected, n_head, piece)
        after = held
        outs.append(held)
    summed = chip_step(jnp.stack(outs), n_head)
    return summed.reshape((-1,) + summed.shape[2:])


def solution(mesh):
    n_ctx = mesh.shape["ctx"]
    n_head = mesh.shape["head"]
    n_zh = 2
    n_xy = n_ctx // n_zh
    devices = np.asarray(mesh.devices).reshape(n_zh, n_xy, n_head)
    inner = Mesh(devices, ("zh", "xy", "head"))
    ctx = ("zh", "xy")
    placed = (P(ctx, "head"), P(ctx, "head"), P(ctx, "head"), P(ctx), P("head", None))
    return jax.shard_map(
        functools.partial(per_device, n_xy, n_head),
        mesh=inner,
        in_specs=placed,
        out_specs=P(("zh", "xy", "head"), None),
        check_vma=False,
    )
```

```python
import functools

import jax
import jax.numpy as jnp
import numpy as np
from jax import lax
from jax.experimental import pallas as pl
from jax.experimental.pallas import tpu as pltpu
from jax.sharding import Mesh, PartitionSpec as P

HEAD_WIDTH = 128
LANES = 128
MOST = 6528
DOCS = 16
NEG = -1e30
CHUNKS = 2


def attn_kernel(
    steps, shard_rows, heads, scale, sc_ref, q_ref, k_ref, v_ref, qs_ref, qp_ref, after_ref, o_ref, m_sc, l_sc, acc_sc
):
    j = pl.program_id(0)
    me = sc_ref[0]
    first = sc_ref[1]
    q_last_start = sc_ref[2]
    shard = me - (steps - 1) + j
    rows = q_ref.shape[0]

    @pl.when(j == 0)
    def _init():
        m_sc[...] = jnp.full(m_sc.shape, NEG, jnp.float32)
        l_sc[...] = jnp.zeros(l_sc.shape, jnp.float32)
        acc_sc[...] = jnp.zeros(acc_sc.shape, jnp.float32)

    def block(masked):
        cols = shard_rows // LANES
        if masked:
            lane = lax.broadcasted_iota(jnp.int32, (rows, LANES), 1)
            allowed = []
            for c in range(cols):
                k_pos = shard * shard_rows + c * LANES + lane
                allowed.append((k_pos >= qs_ref[:, 0:1]) & (k_pos <= qp_ref[:, 0:1]))
        for h in range(heads):
            qh = q_ref[:, h * HEAD_WIDTH:(h + 1) * HEAD_WIDTH]
            s = []
            for c in range(cols):
                s_c = jnp.dot(qh, k_ref[c * LANES:(c + 1) * LANES, :], preferred_element_type=jnp.float32)
                if masked:
                    s_c = jnp.where(allowed[c], s_c, NEG)
                s.append(s_c)
            top = s[0]
            for c in range(1, cols):
                top = jnp.maximum(top, s[c])
            m_prev = m_sc[h]
            m_next = jnp.maximum(m_prev, jnp.max(top, axis=1, keepdims=True))
            m_b = m_next[:, 0:1]
            part = None
            pv = None
            for c in range(cols):
                p = jnp.exp((s[c] - m_b) * scale)
                if masked:
                    p = jnp.where(allowed[c], p, 0.0)
                part = p if part is None else part + p
                term = jnp.dot(
                    p.astype(jnp.bfloat16), v_ref[c * LANES:(c + 1) * LANES, :], preferred_element_type=jnp.float32
                )
                pv = term if pv is None else pv + term
            alpha = jnp.exp((m_prev - m_next) * scale)
            l_sc[h] = alpha * l_sc[h] + part
            acc_sc[h] = alpha[:, 0:1] * acc_sc[h] + pv
            m_sc[h] = m_next

    live = shard >= first
    full = (shard < me) & (shard * shard_rows >= q_last_start)

    @pl.when(live & full)
    def _full():
        block(False)

    @pl.when(live & jnp.logical_not(full))
    def _masked():
        block(True)

    @pl.when(j == steps - 1)
    def _finish():
        for h in range(heads):
            denominator = jnp.sum(l_sc[h], axis=1, keepdims=True)
            o_ref[:, h * HEAD_WIDTH:(h + 1) * HEAD_WIDTH] = (acc_sc[h] / denominator).astype(o_ref.dtype)


def attention(scalars, queries, kv, q_start, q_pos, after, n_xy, shard_rows):
    rows, width = queries.shape
    heads = width // HEAD_WIDTH
    steps = -(-(MOST - 1) // shard_rows) + 1
    scale = HEAD_WIDTH ** (-0.5)

    def index(j, sc, half):
        s = jnp.maximum(sc[0] - (steps - 1) + j, sc[1])
        slot = jnp.where(s // n_xy == sc[3], 0, 1)
        return (s % n_xy, slot, 0, half)

    kernel = functools.partial(attn_kernel, steps, shard_rows, heads, scale)
    return pl.pallas_call(
        kernel,
        out_shape=jax.ShapeDtypeStruct((rows, width), jnp.bfloat16),
        grid_spec=pltpu.PrefetchScalarGridSpec(
            num_scalar_prefetch=1,
            grid=(steps,),
            in_specs=[
                pl.BlockSpec((rows, width), lambda j, sc: (0, 0)),
                pl.BlockSpec((None, None, shard_rows, HEAD_WIDTH), lambda j, sc: index(j, sc, 0)),
                pl.BlockSpec((None, None, shard_rows, HEAD_WIDTH), lambda j, sc: index(j, sc, 1)),
                pl.BlockSpec((rows, LANES), lambda j, sc: (0, 0)),
                pl.BlockSpec((rows, LANES), lambda j, sc: (0, 0)),
                pl.BlockSpec(memory_space=pl.ANY),
            ],
            out_specs=pl.BlockSpec((rows, width), lambda j, sc: (0, 0)),
            scratch_shapes=[
                pltpu.VMEM((heads, rows, LANES), jnp.float32),
                pltpu.VMEM((heads, rows, LANES), jnp.float32),
                pltpu.VMEM((heads, rows, HEAD_WIDTH), jnp.float32),
            ],
        ),
        compiler_params=pltpu.CompilerParams(dimension_semantics=("arbitrary",)),
        cost_estimate=pl.CostEstimate(
            flops=4 * steps * heads * rows * shard_rows * HEAD_WIDTH,
            transcendentals=steps * heads * rows * shard_rows,
            bytes_accessed=steps * shard_rows * 2 * HEAD_WIDTH * 2 + 2 * rows * width * 2,
        ),
    )(scalars, queries, kv, kv, q_start, q_pos, after)


def sum_over_heads(projected, n_head, piece):
    me_head = lax.axis_index("head")
    held = projected.reshape((n_head // 2, 2, piece) + projected.shape[1:]).astype(jnp.float32)
    core = me_head % 2
    keep = lax.dynamic_index_in_dim(held, core, axis=1, keepdims=False)
    send = lax.dynamic_index_in_dim(held, 1 - core, axis=1, keepdims=False)
    got = lax.ppermute(send.astype(jnp.bfloat16), "head", perm=[(i, i ^ 1) for i in range(n_head)])
    held = keep + got.astype(jnp.float32)
    chip = me_head // 2
    total = lax.dynamic_index_in_dim(held, chip, axis=0, keepdims=False)
    for k in range(1, n_head // 2):
        send = lax.dynamic_index_in_dim(held, chip ^ k, axis=0, keepdims=False)
        got = lax.ppermute(send.astype(jnp.bfloat16), "head", perm=[(i, i ^ (2 * k)) for i in range(n_head)])
        total = total + got.astype(jnp.float32)
    return total.astype(jnp.bfloat16)


def per_device(n_xy, n_head, queries, key_matrix, value_matrix, doc_ids, out_weight):
    rows = queries.shape[0]
    zh = lax.axis_index("zh")
    me = zh * n_xy + lax.axis_index("xy")

    width = key_matrix.shape[1]
    k_t = key_matrix.T.reshape(width, rows // LANES, LANES).transpose(1, 0, 2).reshape(rows, width)
    kv = jnp.concatenate([k_t, value_matrix], axis=1)
    lanes = kv.shape[1]
    tile = 8
    ids = jnp.full((tile * lanes,), -1.0, jnp.float32).at[:rows].set(doc_ids.astype(jnp.float32))
    block = jnp.concatenate([kv, ids.reshape(tile, lanes).astype(kv.dtype)], axis=0)

    partner = lax.ppermute(block, "zh", perm=[(0, 1), (1, 0)])
    pair = jnp.stack([block, partner])
    gathered = lax.all_gather(pair, "xy")

    id_rows = gathered[:, :, rows:, :].astype(jnp.float32)
    docs = jnp.arange(DOCS, dtype=jnp.float32)
    counts = jnp.sum((id_rows[..., None] == docs).astype(jnp.float32), axis=(0, 1, 2, 3))
    below = (jnp.arange(DOCS, dtype=jnp.int32)[None, :] < doc_ids[:, None]).astype(jnp.float32)
    q_start = jnp.sum(below * counts[None, :], axis=1).astype(jnp.int32)
    q_pos = me * rows + jnp.arange(rows, dtype=jnp.int32)

    per_head = rows // n_head
    piece = per_head // CHUNKS

    def chunk_of(x, c):
        x = x.reshape((n_head, CHUNKS, piece) + x.shape[1:])[:, c]
        return x.reshape((n_head * piece,) + x.shape[2:])

    outs = []
    after = jnp.zeros((8, LANES), jnp.bfloat16)
    for c in range(CHUNKS):
        qs_c = chunk_of(q_start, c)
        qp_c = chunk_of(q_pos, c)
        first = jnp.maximum(qs_c[0] // rows, 0)
        scalars = jnp.stack([me, first, qs_c[-1], zh]).astype(jnp.int32)
        attended = attention(
            scalars,
            chunk_of(queries, c),
            gathered,
            jnp.broadcast_to(qs_c[:, None], (qs_c.shape[0], LANES)),
            jnp.broadcast_to(qp_c[:, None], (qp_c.shape[0], LANES)),
            after,
            n_xy,
            rows,
        )
        projected = jnp.dot(attended, out_weight, preferred_element_type=jnp.float32).astype(jnp.bfloat16)
        after = projected
        if c < CHUNKS - 1:
            outs.append(lax.psum_scatter(projected, "head", scatter_dimension=0, tiled=True))
        else:
            *outs, projected = lax.optimization_barrier((*outs, projected))
            outs.append(sum_over_heads(projected, n_head, piece))
    return jnp.concatenate(outs, axis=0)


def solution(mesh):
    n_ctx = mesh.shape["ctx"]
    n_head = mesh.shape["head"]
    n_zh = 2
    n_xy = n_ctx // n_zh
    devices = np.asarray(mesh.devices).reshape(n_zh, n_xy, n_head)
    inner = Mesh(devices, ("zh", "xy", "head"))
    ctx = ("zh", "xy")
    placed = (P(ctx, "head"), P(ctx, "head"), P(ctx, "head"), P(ctx), P("head", None))
    return jax.shard_map(
        functools.partial(per_device, n_xy, n_head),
        mesh=inner,
        in_specs=placed,
        out_specs=P(("zh", "xy", "head"), None),
        check_vma=False,
    )
```

```python
import functools

import jax
import jax.numpy as jnp
import numpy as np
from jax import lax
from jax.experimental import pallas as pl
from jax.experimental.pallas import tpu as pltpu
from jax.sharding import Mesh, PartitionSpec as P

HEAD_WIDTH = 128
LANES = 128
MOST = 6528
DOCS = 16
NEG = -1e30
CHUNKS = 2


def attn_kernel(
    steps, shard_rows, heads, scale, at, sc_ref, q_ref, k_ref, v_ref, qs_ref, qp_ref, after_ref, o_ref, m_sc, l_sc, acc_sc
):
    j = pl.program_id(0)
    me = sc_ref[at]
    first = sc_ref[at + 1]
    q_last_start = sc_ref[at + 2]
    shard = me - (steps - 1) + j
    rows = q_ref.shape[0]

    @pl.when(j == 0)
    def _init():
        m_sc[...] = jnp.full(m_sc.shape, NEG, jnp.float32)
        l_sc[...] = jnp.zeros(l_sc.shape, jnp.float32)
        acc_sc[...] = jnp.zeros(acc_sc.shape, jnp.float32)

    def block(masked):
        cols = shard_rows // LANES
        if masked:
            lane = lax.broadcasted_iota(jnp.int32, (rows, LANES), 1)
            q_start = qs_ref[...].reshape(rows, LANES)[:, 0:1]
            q_pos = qp_ref[...].reshape(rows, LANES)[:, 0:1]
            allowed = []
            for c in range(cols):
                k_pos = shard * shard_rows + c * LANES + lane
                allowed.append((k_pos >= q_start) & (k_pos <= q_pos))
        for h in range(heads):
            qh = q_ref[:, h * HEAD_WIDTH:(h + 1) * HEAD_WIDTH]
            s = []
            for c in range(cols):
                s_c = jnp.dot(qh, k_ref[c * LANES:(c + 1) * LANES, :], preferred_element_type=jnp.float32)
                if masked:
                    s_c = jnp.where(allowed[c], s_c, NEG)
                s.append(s_c)
            top = s[0]
            for c in range(1, cols):
                top = jnp.maximum(top, s[c])
            m_prev = m_sc[h]
            m_next = jnp.maximum(m_prev, jnp.max(top, axis=1, keepdims=True))
            m_b = m_next[:, 0:1]
            part = None
            pv = None
            for c in range(cols):
                p = jnp.exp((s[c] - m_b) * scale)
                if masked:
                    p = jnp.where(allowed[c], p, 0.0)
                part = p if part is None else part + p
                term = jnp.dot(
                    p.astype(jnp.bfloat16), v_ref[c * LANES:(c + 1) * LANES, :], preferred_element_type=jnp.float32
                )
                pv = term if pv is None else pv + term
            alpha = jnp.exp((m_prev - m_next) * scale)
            l_sc[h] = alpha * l_sc[h] + part
            acc_sc[h] = alpha[:, 0:1] * acc_sc[h] + pv
            m_sc[h] = m_next

    live = shard >= first
    full = (shard < me) & (shard * shard_rows >= q_last_start)

    @pl.when(live & full)
    def _full():
        block(False)

    @pl.when(live & jnp.logical_not(full))
    def _masked():
        block(True)

    @pl.when(j == steps - 1)
    def _finish():
        for h in range(heads):
            denominator = jnp.sum(l_sc[h], axis=1, keepdims=True)
            o_ref[:, h * HEAD_WIDTH:(h + 1) * HEAD_WIDTH] = (acc_sc[h] / denominator).astype(o_ref.dtype)


def attention(scalars, chunk, queries, kv, q_start, q_pos, after, n_xy, shard_rows):
    rows, width = queries.shape
    heads = width // HEAD_WIDTH
    steps = -(-(MOST - 1) // shard_rows) + 1
    scale = HEAD_WIDTH ** (-0.5)

    at = 4 * chunk

    def index(j, sc, half):
        s = jnp.maximum(sc[at] - (steps - 1) + j, sc[at + 1])
        slot = jnp.where(s // n_xy == sc[at + 3], 0, 1)
        return (s % n_xy, slot, 0, half)

    groups, _, piece, _ = q_start.shape
    kernel = functools.partial(attn_kernel, steps, shard_rows, heads, scale, at)
    return pl.pallas_call(
        kernel,
        out_shape=jax.ShapeDtypeStruct((rows, width), jnp.bfloat16),
        grid_spec=pltpu.PrefetchScalarGridSpec(
            num_scalar_prefetch=1,
            grid=(steps,),
            in_specs=[
                pl.BlockSpec((rows, width), lambda j, sc: (0, 0)),
                pl.BlockSpec((None, None, shard_rows, HEAD_WIDTH), lambda j, sc: index(j, sc, 0)),
                pl.BlockSpec((None, None, shard_rows, HEAD_WIDTH), lambda j, sc: index(j, sc, 1)),
                pl.BlockSpec((groups, None, piece, LANES), lambda j, sc: (0, chunk, 0, 0)),
                pl.BlockSpec((groups, None, piece, LANES), lambda j, sc: (0, chunk, 0, 0)),
                pl.BlockSpec(memory_space=pl.ANY),
            ],
            out_specs=pl.BlockSpec((rows, width), lambda j, sc: (0, 0)),
            scratch_shapes=[
                pltpu.VMEM((heads, rows, LANES), jnp.float32),
                pltpu.VMEM((heads, rows, LANES), jnp.float32),
                pltpu.VMEM((heads, rows, HEAD_WIDTH), jnp.float32),
            ],
        ),
        compiler_params=pltpu.CompilerParams(dimension_semantics=("arbitrary",)),
        cost_estimate=pl.CostEstimate(
            flops=4 * steps * heads * rows * shard_rows * HEAD_WIDTH,
            transcendentals=steps * heads * rows * shard_rows,
            bytes_accessed=steps * shard_rows * 2 * HEAD_WIDTH * 2 + 2 * rows * width * 2,
        ),
    )(scalars, queries, kv, kv, q_start, q_pos, after)


def sum_over_heads(projected, n_head, piece):
    me_head = lax.axis_index("head")
    held = projected.reshape((n_head // 2, 2, piece) + projected.shape[1:]).astype(jnp.float32)
    core = me_head % 2
    keep = lax.dynamic_index_in_dim(held, core, axis=1, keepdims=False)
    send = lax.dynamic_index_in_dim(held, 1 - core, axis=1, keepdims=False)
    got = lax.ppermute(send.astype(jnp.bfloat16), "head", perm=[(i, i ^ 1) for i in range(n_head)])
    held = keep + got.astype(jnp.float32)
    chip = me_head // 2
    total = lax.dynamic_index_in_dim(held, chip, axis=0, keepdims=False)
    for k in range(1, n_head // 2):
        send = lax.dynamic_index_in_dim(held, chip ^ k, axis=0, keepdims=False)
        got = lax.ppermute(send.astype(jnp.bfloat16), "head", perm=[(i, i ^ (2 * k)) for i in range(n_head)])
        total = total + got.astype(jnp.float32)
    return total.astype(jnp.bfloat16)


def per_device(n_xy, n_head, queries, key_matrix, value_matrix, doc_ids, out_weight):
    rows = queries.shape[0]
    zh = lax.axis_index("zh")
    me = zh * n_xy + lax.axis_index("xy")

    width = key_matrix.shape[1]
    k_t = key_matrix.T.reshape(width, rows // LANES, LANES).transpose(1, 0, 2).reshape(rows, width)
    kv = jnp.concatenate([k_t, value_matrix], axis=1)
    lanes = kv.shape[1]
    tile = 8
    ids = jnp.full((tile * lanes,), -1.0, jnp.float32).at[:rows].set(doc_ids.astype(jnp.float32))
    block = jnp.concatenate([kv, ids.reshape(tile, lanes).astype(kv.dtype)], axis=0)

    partner = lax.ppermute(block, "zh", perm=[(0, 1), (1, 0)])
    pair = jnp.stack([block, partner])
    gathered = lax.all_gather(pair, "xy")

    id_rows = gathered[:, :, rows:, :].astype(jnp.float32)
    docs = jnp.arange(DOCS, dtype=jnp.float32)
    counts = jnp.sum((id_rows[..., None] == docs).astype(jnp.float32), axis=(0, 1, 2, 3))
    below = (jnp.arange(DOCS, dtype=jnp.int32)[None, :] < doc_ids[:, None]).astype(jnp.float32)
    q_start = jnp.sum(below * counts[None, :], axis=1).astype(jnp.int32)
    q_pos = me * rows + jnp.arange(rows, dtype=jnp.int32)

    per_head = rows // n_head
    piece = per_head // CHUNKS

    def chunk_of(x, c):
        x = x.reshape((n_head, CHUNKS, piece) + x.shape[1:])[:, c]
        return x.reshape((n_head * piece,) + x.shape[2:])

    def rows_view(x):
        return jnp.broadcast_to(x[:, None], (rows, LANES)).reshape(n_head, CHUNKS, piece, LANES)

    q_start_b = rows_view(q_start)
    q_pos_b = rows_view(q_pos)
    q_start_c = q_start.reshape(n_head, CHUNKS, piece)
    firsts = jnp.maximum(q_start_c[0, :, 0] // rows, 0)
    lasts = q_start_c[n_head - 1, :, piece - 1]
    scalars = jnp.stack(
        [jnp.full((CHUNKS,), me), firsts, lasts, jnp.full((CHUNKS,), zh)], axis=1
    ).reshape(-1).astype(jnp.int32)

    outs = []
    after = gathered
    for c in range(CHUNKS):
        attended = attention(scalars, c, chunk_of(queries, c), gathered, q_start_b, q_pos_b, after, n_xy, rows)
        projected = jnp.dot(attended, out_weight, preferred_element_type=jnp.float32).astype(jnp.bfloat16)
        after = projected
        if c < CHUNKS - 1:
            outs.append(lax.psum_scatter(projected, "head", scatter_dimension=0, tiled=True))
        else:
            *outs, projected = lax.optimization_barrier((*outs, projected))
            outs.append(sum_over_heads(projected, n_head, piece))
    return jnp.concatenate(outs, axis=0)


def solution(mesh):
    n_ctx = mesh.shape["ctx"]
    n_head = mesh.shape["head"]
    n_zh = 2
    n_xy = n_ctx // n_zh
    devices = np.asarray(mesh.devices).reshape(n_zh, n_xy, n_head)
    inner = Mesh(devices, ("zh", "xy", "head"))
    ctx = ("zh", "xy")
    placed = (P(ctx, "head"), P(ctx, "head"), P(ctx, "head"), P(ctx), P("head", None))
    return jax.shard_map(
        functools.partial(per_device, n_xy, n_head),
        mesh=inner,
        in_specs=placed,
        out_specs=P(("zh", "xy", "head"), None),
        check_vma=False,
    )
```

```python
import functools

import jax
import jax.numpy as jnp
import numpy as np
from jax import lax
from jax.experimental import pallas as pl
from jax.experimental.pallas import tpu as pltpu
from jax.sharding import Mesh, PartitionSpec as P

HEAD_WIDTH = 128
LANES = 128
MOST = 6528
DOCS = 16
NEG = -1e30
CHUNKS = 2


def attn_kernel(
    steps, shard_rows, heads, scale, at, sc_ref, q_ref, k_ref, v_ref, qs_ref, qp_ref, after_ref, o_ref, m_sc, l_sc, acc_sc
):
    j = pl.program_id(0)
    me = sc_ref[at]
    first = sc_ref[at + 1]
    q_last_start = sc_ref[at + 2]
    shard = me - (steps - 1) + j
    rows = q_ref.shape[0]

    @pl.when(j == 0)
    def _init():
        m_sc[...] = jnp.full(m_sc.shape, NEG, jnp.float32)
        l_sc[...] = jnp.zeros(l_sc.shape, jnp.float32)
        acc_sc[...] = jnp.zeros(acc_sc.shape, jnp.float32)

    def block(masked):
        cols = shard_rows // LANES
        if masked:
            lane = lax.broadcasted_iota(jnp.int32, (rows, LANES), 1)
            q_start = qs_ref[...].reshape(rows, LANES)[:, 0:1]
            q_pos = qp_ref[...].reshape(rows, LANES)[:, 0:1]
            allowed = []
            for c in range(cols):
                k_pos = shard * shard_rows + c * LANES + lane
                allowed.append((k_pos >= q_start) & (k_pos <= q_pos))
        for h in range(heads):
            qh = q_ref[:, h * HEAD_WIDTH:(h + 1) * HEAD_WIDTH]
            s = []
            for c in range(cols):
                s_c = jnp.dot(qh, k_ref[c * LANES:(c + 1) * LANES, :], preferred_element_type=jnp.float32)
                if masked:
                    s_c = jnp.where(allowed[c], s_c, NEG)
                s.append(s_c)
            top = s[0]
            for c in range(1, cols):
                top = jnp.maximum(top, s[c])
            m_prev = m_sc[h]
            m_next = jnp.maximum(m_prev, jnp.max(top, axis=1, keepdims=True))
            m_b = m_next[:, 0:1]
            part = None
            pv = None
            for c in range(cols):
                p = jnp.exp((s[c] - m_b) * scale)
                if masked:
                    p = jnp.where(allowed[c], p, 0.0)
                part = p if part is None else part + p
                term = jnp.dot(
                    p.astype(jnp.bfloat16), v_ref[c * LANES:(c + 1) * LANES, :], preferred_element_type=jnp.float32
                )
                pv = term if pv is None else pv + term
            alpha = jnp.exp((m_prev - m_next) * scale)
            l_sc[h] = alpha * l_sc[h] + part
            acc_sc[h] = alpha[:, 0:1] * acc_sc[h] + pv
            m_sc[h] = m_next

    live = shard >= first
    full = (shard < me) & (shard * shard_rows >= q_last_start)

    @pl.when(live & full)
    def _full():
        block(False)

    @pl.when(live & jnp.logical_not(full))
    def _masked():
        block(True)

    @pl.when(j == steps - 1)
    def _finish():
        for h in range(heads):
            denominator = jnp.sum(l_sc[h], axis=1, keepdims=True)
            o_ref[:, h * HEAD_WIDTH:(h + 1) * HEAD_WIDTH] = (acc_sc[h] / denominator).astype(o_ref.dtype)


def attention(scalars, chunk, queries, kv, q_start, q_pos, after, n_xy, shard_rows):
    rows, width = queries.shape
    heads = width // HEAD_WIDTH
    steps = -(-(MOST - 1) // shard_rows) + 1
    scale = HEAD_WIDTH ** (-0.5)

    at = 4 * chunk

    def index(j, sc, half):
        s = jnp.maximum(sc[at] - (steps - 1) + j, sc[at + 1])
        slot = jnp.where(s // n_xy == sc[at + 3], 0, 1)
        return (s % n_xy, slot, 0, half)

    groups, _, piece, _ = q_start.shape
    kernel = functools.partial(attn_kernel, steps, shard_rows, heads, scale, at)
    return pl.pallas_call(
        kernel,
        out_shape=jax.ShapeDtypeStruct((rows, width), jnp.bfloat16),
        grid_spec=pltpu.PrefetchScalarGridSpec(
            num_scalar_prefetch=1,
            grid=(steps,),
            in_specs=[
                pl.BlockSpec((rows, width), lambda j, sc: (0, 0)),
                pl.BlockSpec((None, None, shard_rows, HEAD_WIDTH), lambda j, sc: index(j, sc, 0)),
                pl.BlockSpec((None, None, shard_rows, HEAD_WIDTH), lambda j, sc: index(j, sc, 1)),
                pl.BlockSpec((groups, None, piece, LANES), lambda j, sc: (0, chunk, 0, 0)),
                pl.BlockSpec((groups, None, piece, LANES), lambda j, sc: (0, chunk, 0, 0)),
                pl.BlockSpec(memory_space=pl.ANY),
            ],
            out_specs=pl.BlockSpec((rows, width), lambda j, sc: (0, 0)),
            scratch_shapes=[
                pltpu.VMEM((heads, rows, LANES), jnp.float32),
                pltpu.VMEM((heads, rows, LANES), jnp.float32),
                pltpu.VMEM((heads, rows, HEAD_WIDTH), jnp.float32),
            ],
        ),
        compiler_params=pltpu.CompilerParams(dimension_semantics=("arbitrary",)),
        cost_estimate=pl.CostEstimate(
            flops=4 * steps * heads * rows * shard_rows * HEAD_WIDTH,
            transcendentals=steps * heads * rows * shard_rows,
            bytes_accessed=steps * shard_rows * 2 * HEAD_WIDTH * 2 + 2 * rows * width * 2,
        ),
    )(scalars, queries, kv, kv, q_start, q_pos, after)


def core_step(projected, n_head, piece):
    me_head = lax.axis_index("head")
    held = projected.reshape((n_head // 2, 2, piece) + projected.shape[1:])
    core = me_head % 2
    keep = lax.dynamic_index_in_dim(held, core, axis=1, keepdims=False)
    send = lax.dynamic_index_in_dim(held, 1 - core, axis=1, keepdims=False)
    got = lax.ppermute(send, "head", perm=[(i, i ^ 1) for i in range(n_head)])
    return keep.astype(jnp.float32) + got.astype(jnp.float32)


def chip_step(held, n_head):
    chip = lax.axis_index("head") // 2
    total = lax.dynamic_index_in_dim(held, chip, axis=0, keepdims=False)
    for k in range(1, n_head // 2):
        send = lax.dynamic_index_in_dim(held, chip ^ k, axis=0, keepdims=False)
        got = lax.ppermute(send.astype(jnp.bfloat16), "head", perm=[(i, i ^ (2 * k)) for i in range(n_head)])
        total = total + got.astype(jnp.float32)
    return total.astype(jnp.bfloat16)


def per_device(n_xy, n_head, queries, key_matrix, value_matrix, doc_ids, out_weight):
    rows = queries.shape[0]
    zh = lax.axis_index("zh")
    me = zh * n_xy + lax.axis_index("xy")

    width = key_matrix.shape[1]
    k_t = key_matrix.T.reshape(width, rows // LANES, LANES).transpose(1, 0, 2).reshape(rows, width)
    kv = jnp.concatenate([k_t, value_matrix], axis=1)
    lanes = kv.shape[1]
    tile = 8
    ids = jnp.full((tile * lanes,), -1.0, jnp.float32).at[:rows].set(doc_ids.astype(jnp.float32))
    block = jnp.concatenate([kv, ids.reshape(tile, lanes).astype(kv.dtype)], axis=0)

    partner = lax.ppermute(block, "zh", perm=[(0, 1), (1, 0)])
    pair = jnp.stack([block, partner])
    gathered = lax.all_gather(pair, "xy")

    id_rows = gathered[:, :, rows:, :].astype(jnp.float32)
    docs = jnp.arange(DOCS, dtype=jnp.float32)
    counts = jnp.sum((id_rows[..., None] == docs).astype(jnp.float32), axis=(0, 1, 2, 3))
    below = (jnp.arange(DOCS, dtype=jnp.int32)[None, :] < doc_ids[:, None]).astype(jnp.float32)
    q_start = jnp.sum(below * counts[None, :], axis=1).astype(jnp.int32)
    q_pos = me * rows + jnp.arange(rows, dtype=jnp.int32)

    per_head = rows // n_head
    piece = per_head // CHUNKS

    def chunk_of(x, c):
        x = x.reshape((n_head, CHUNKS, piece) + x.shape[1:])[:, c]
        return x.reshape((n_head * piece,) + x.shape[2:])

    def rows_view(x):
        return jnp.broadcast_to(x[:, None], (rows, LANES)).reshape(n_head, CHUNKS, piece, LANES)

    q_start_b = rows_view(q_start)
    q_pos_b = rows_view(q_pos)
    q_start_c = q_start.reshape(n_head, CHUNKS, piece)
    firsts = jnp.maximum(q_start_c[0, :, 0] // rows, 0)
    lasts = q_start_c[n_head - 1, :, piece - 1]
    scalars = jnp.stack(
        [jnp.full((CHUNKS,), me), firsts, lasts, jnp.full((CHUNKS,), zh)], axis=1
    ).reshape(-1).astype(jnp.int32)

    outs = []
    after = gathered
    for c in range(CHUNKS):
        attended = attention(scalars, c, chunk_of(queries, c), gathered, q_start_b, q_pos_b, after, n_xy, rows)
        projected = jnp.dot(attended, out_weight, preferred_element_type=jnp.float32).astype(jnp.bfloat16)
        after = projected
        if c < CHUNKS - 1:
            outs.append(lax.psum_scatter(projected, "head", scatter_dimension=0, tiled=True))
        else:
            held = core_step(projected, n_head, piece)
            *outs, held = lax.optimization_barrier((*outs, held))
            outs.append(chip_step(held, n_head))
    return jnp.concatenate(outs, axis=0)


def solution(mesh):
    n_ctx = mesh.shape["ctx"]
    n_head = mesh.shape["head"]
    n_zh = 2
    n_xy = n_ctx // n_zh
    devices = np.asarray(mesh.devices).reshape(n_zh, n_xy, n_head)
    inner = Mesh(devices, ("zh", "xy", "head"))
    ctx = ("zh", "xy")
    placed = (P(ctx, "head"), P(ctx, "head"), P(ctx, "head"), P(ctx), P("head", None))
    return jax.shard_map(
        functools.partial(per_device, n_xy, n_head),
        mesh=inner,
        in_specs=placed,
        out_specs=P(("zh", "xy", "head"), None),
        check_vma=False,
    )
```

```python
import functools
import math

import jax
import jax.numpy as jnp
import numpy as np
from jax import lax
from jax.experimental import pallas as pl
from jax.experimental.pallas import tpu as pltpu
from jax.sharding import Mesh, PartitionSpec as P

HEAD_WIDTH = 128
LANES = 128
MOST = 6528
DOCS = 16
NEG = -1e30
CHUNKS = 2


def attn_kernel(
    steps, shard_rows, heads, scale, at, sc_ref, q_ref, k_ref, v_ref, qs_ref, qp_ref, after_ref, o_ref, m_sc, l_sc, acc_sc
):
    j = pl.program_id(0)
    me = sc_ref[at]
    first = sc_ref[at + 1]
    q_last_start = sc_ref[at + 2]
    shard = me - (steps - 1) + j
    rows = q_ref.shape[0]

    @pl.when(j == 0)
    def _init():
        m_sc[...] = jnp.full(m_sc.shape, NEG, jnp.float32)
        l_sc[...] = jnp.zeros(l_sc.shape, jnp.float32)
        acc_sc[...] = jnp.zeros(acc_sc.shape, jnp.float32)

    def block(masked):
        cols = shard_rows // LANES
        if masked:
            lane = lax.broadcasted_iota(jnp.int32, (rows, LANES), 1)
            q_start = qs_ref[...].reshape(rows, LANES)[:, 0:1]
            q_pos = qp_ref[...].reshape(rows, LANES)[:, 0:1]
            allowed = []
            for c in range(cols):
                k_pos = shard * shard_rows + c * LANES + lane
                allowed.append((k_pos >= q_start) & (k_pos <= q_pos))
        for h in range(heads):
            qh = q_ref[:, h * HEAD_WIDTH:(h + 1) * HEAD_WIDTH]
            s = []
            for c in range(cols):
                s_c = jnp.dot(qh, k_ref[c * LANES:(c + 1) * LANES, :], preferred_element_type=jnp.float32)
                if masked:
                    s_c = jnp.where(allowed[c], s_c, NEG)
                s.append(s_c)
            top = s[0]
            for c in range(1, cols):
                top = jnp.maximum(top, s[c])
            m_prev = m_sc[h]
            m_next = jnp.maximum(m_prev, jnp.max(top, axis=1, keepdims=True))
            m_b = m_next[:, 0:1]
            part = None
            pv = None
            for c in range(cols):
                p = jnp.exp2((s[c] - m_b) * scale)
                if masked:
                    p = jnp.where(allowed[c], p, 0.0)
                part = p if part is None else part + p
                term = jnp.dot(
                    p.astype(jnp.bfloat16), v_ref[c * LANES:(c + 1) * LANES, :], preferred_element_type=jnp.float32
                )
                pv = term if pv is None else pv + term
            alpha = jnp.exp2((m_prev - m_next) * scale)
            l_sc[h] = alpha * l_sc[h] + part
            acc_sc[h] = alpha[:, 0:1] * acc_sc[h] + pv
            m_sc[h] = m_next

    live = shard >= first
    full = (shard < me) & (shard * shard_rows >= q_last_start)

    @pl.when(live & full)
    def _full():
        block(False)

    @pl.when(live & jnp.logical_not(full))
    def _masked():
        block(True)

    @pl.when(j == steps - 1)
    def _finish():
        for h in range(heads):
            denominator = jnp.sum(l_sc[h], axis=1, keepdims=True)
            o_ref[:, h * HEAD_WIDTH:(h + 1) * HEAD_WIDTH] = (acc_sc[h] / denominator).astype(o_ref.dtype)


def attention(scalars, chunk, queries, kv, q_start, q_pos, after, n_xy, shard_rows):
    rows, width = queries.shape
    heads = width // HEAD_WIDTH
    steps = -(-(MOST - 1) // shard_rows) + 1
    scale = HEAD_WIDTH ** (-0.5) * math.log2(math.e)

    at = 4 * chunk

    def index(j, sc, half):
        s = jnp.maximum(sc[at] - (steps - 1) + j, sc[at + 1])
        slot = jnp.where(s // n_xy == sc[at + 3], 0, 1)
        return (s % n_xy, slot, 0, half)

    groups, _, piece, _ = q_start.shape
    kernel = functools.partial(attn_kernel, steps, shard_rows, heads, scale, at)
    return pl.pallas_call(
        kernel,
        out_shape=jax.ShapeDtypeStruct((rows, width), jnp.bfloat16),
        grid_spec=pltpu.PrefetchScalarGridSpec(
            num_scalar_prefetch=1,
            grid=(steps,),
            in_specs=[
                pl.BlockSpec((rows, width), lambda j, sc: (0, 0)),
                pl.BlockSpec((None, None, shard_rows, HEAD_WIDTH), lambda j, sc: index(j, sc, 0)),
                pl.BlockSpec((None, None, shard_rows, HEAD_WIDTH), lambda j, sc: index(j, sc, 1)),
                pl.BlockSpec((groups, None, piece, LANES), lambda j, sc: (0, chunk, 0, 0)),
                pl.BlockSpec((groups, None, piece, LANES), lambda j, sc: (0, chunk, 0, 0)),
                pl.BlockSpec(memory_space=pl.ANY),
            ],
            out_specs=pl.BlockSpec((rows, width), lambda j, sc: (0, 0)),
            scratch_shapes=[
                pltpu.VMEM((heads, rows, LANES), jnp.float32),
                pltpu.VMEM((heads, rows, LANES), jnp.float32),
                pltpu.VMEM((heads, rows, HEAD_WIDTH), jnp.float32),
            ],
        ),
        compiler_params=pltpu.CompilerParams(dimension_semantics=("arbitrary",)),
        cost_estimate=pl.CostEstimate(
            flops=4 * steps * heads * rows * shard_rows * HEAD_WIDTH,
            transcendentals=steps * heads * rows * shard_rows,
            bytes_accessed=steps * shard_rows * 2 * HEAD_WIDTH * 2 + 2 * rows * width * 2,
        ),
    )(scalars, queries, kv, kv, q_start, q_pos, after)


def core_step(projected, n_head, piece):
    me_head = lax.axis_index("head")
    held = projected.reshape((n_head // 2, 2, piece) + projected.shape[1:])
    core = me_head % 2
    keep = lax.dynamic_index_in_dim(held, core, axis=1, keepdims=False)
    send = lax.dynamic_index_in_dim(held, 1 - core, axis=1, keepdims=False)
    got = lax.ppermute(send, "head", perm=[(i, i ^ 1) for i in range(n_head)])
    return keep.astype(jnp.float32) + got.astype(jnp.float32)


def chip_step(held, n_head):
    chip = lax.axis_index("head") // 2
    total = lax.dynamic_index_in_dim(held, chip, axis=0, keepdims=False)
    for k in range(1, n_head // 2):
        send = lax.dynamic_index_in_dim(held, chip ^ k, axis=0, keepdims=False)
        got = lax.ppermute(send.astype(jnp.bfloat16), "head", perm=[(i, i ^ (2 * k)) for i in range(n_head)])
        total = total + got.astype(jnp.float32)
    return total.astype(jnp.bfloat16)


def per_device(n_xy, n_head, queries, key_matrix, value_matrix, doc_ids, out_weight):
    rows = queries.shape[0]
    zh = lax.axis_index("zh")
    me = zh * n_xy + lax.axis_index("xy")

    width = key_matrix.shape[1]
    k_t = key_matrix.T.reshape(width, rows // LANES, LANES).transpose(1, 0, 2).reshape(rows, width)
    kv = jnp.concatenate([k_t, value_matrix], axis=1)
    lanes = kv.shape[1]
    tile = 8
    ids = jnp.full((tile * lanes,), -1.0, jnp.float32).at[:rows].set(doc_ids.astype(jnp.float32))
    block = jnp.concatenate([kv, ids.reshape(tile, lanes).astype(kv.dtype)], axis=0)

    partner = lax.ppermute(block, "zh", perm=[(0, 1), (1, 0)])
    pair = jnp.stack([block, partner])
    gathered = lax.all_gather(pair, "xy")

    id_rows = gathered[:, :, rows:, :].astype(jnp.float32)
    docs = jnp.arange(DOCS, dtype=jnp.float32)
    counts = jnp.sum((id_rows[..., None] == docs).astype(jnp.float32), axis=(0, 1, 2, 3))
    below = (jnp.arange(DOCS, dtype=jnp.int32)[None, :] < doc_ids[:, None]).astype(jnp.float32)
    q_start = jnp.sum(below * counts[None, :], axis=1).astype(jnp.int32)
    q_pos = me * rows + jnp.arange(rows, dtype=jnp.int32)

    per_head = rows // n_head
    piece = per_head // CHUNKS

    def chunk_of(x, c):
        x = x.reshape((n_head, CHUNKS, piece) + x.shape[1:])[:, c]
        return x.reshape((n_head * piece,) + x.shape[2:])

    def rows_view(x):
        return jnp.broadcast_to(x[:, None], (rows, LANES)).reshape(n_head, CHUNKS, piece, LANES)

    q_start_b = rows_view(q_start)
    q_pos_b = rows_view(q_pos)
    q_start_c = q_start.reshape(n_head, CHUNKS, piece)
    firsts = jnp.maximum(q_start_c[0, :, 0] // rows, 0)
    lasts = q_start_c[n_head - 1, :, piece - 1]
    scalars = jnp.stack(
        [jnp.full((CHUNKS,), me), firsts, lasts, jnp.full((CHUNKS,), zh)], axis=1
    ).reshape(-1).astype(jnp.int32)

    outs = []
    after = gathered
    for c in range(CHUNKS):
        attended = attention(scalars, c, chunk_of(queries, c), gathered, q_start_b, q_pos_b, after, n_xy, rows)
        projected = jnp.dot(attended, out_weight, preferred_element_type=jnp.float32).astype(jnp.bfloat16)
        after = projected
        if c < CHUNKS - 1:
            outs.append(lax.psum_scatter(projected, "head", scatter_dimension=0, tiled=True))
        else:
            held = core_step(projected, n_head, piece)
            *outs, held = lax.optimization_barrier((*outs, held))
            outs.append(chip_step(held, n_head))
    return jnp.concatenate(outs, axis=0)


def solution(mesh):
    n_ctx = mesh.shape["ctx"]
    n_head = mesh.shape["head"]
    n_zh = 2
    n_xy = n_ctx // n_zh
    devices = np.asarray(mesh.devices).reshape(n_zh, n_xy, n_head)
    inner = Mesh(devices, ("zh", "xy", "head"))
    ctx = ("zh", "xy")
    placed = (P(ctx, "head"), P(ctx, "head"), P(ctx, "head"), P(ctx), P("head", None))
    return jax.shard_map(
        functools.partial(per_device, n_xy, n_head),
        mesh=inner,
        in_specs=placed,
        out_specs=P(("zh", "xy", "head"), None),
        check_vma=False,
    )
```

```python
import functools

import jax
import jax.numpy as jnp
import numpy as np
from jax import lax
from jax.experimental import pallas as pl
from jax.experimental.pallas import tpu as pltpu
from jax.sharding import Mesh, PartitionSpec as P

HEAD_WIDTH = 128
LANES = 128
MOST = 6528
DOCS = 16
NEG = -1e30
CHUNKS = 2


def attn_kernel(
    steps, per_step, shard_rows, heads, scale, at,
    sc_ref, q_ref, k0_ref, v0_ref, k1_ref, v1_ref, qs_ref, qp_ref, after_ref, o_ref, m_sc, l_sc, acc_sc,
):
    j = pl.program_id(0)
    me = sc_ref[at]
    first = sc_ref[at + 1]
    q_last_start = sc_ref[at + 2]
    rows = q_ref.shape[0]
    grid_steps = steps // per_step

    @pl.when(j == 0)
    def _init():
        m_sc[...] = jnp.full(m_sc.shape, NEG, jnp.float32)
        l_sc[...] = jnp.zeros(l_sc.shape, jnp.float32)
        acc_sc[...] = jnp.zeros(acc_sc.shape, jnp.float32)

    def block(masked, shard, k_ref, v_ref):
        cols = shard_rows // LANES
        if masked:
            lane = lax.broadcasted_iota(jnp.int32, (rows, LANES), 1)
            q_start = qs_ref[...].reshape(rows, LANES)[:, 0:1]
            q_pos = qp_ref[...].reshape(rows, LANES)[:, 0:1]
            allowed = []
            for c in range(cols):
                k_pos = shard * shard_rows + c * LANES + lane
                allowed.append((k_pos >= q_start) & (k_pos <= q_pos))
        for h in range(heads):
            qh = q_ref[:, h * HEAD_WIDTH:(h + 1) * HEAD_WIDTH]
            s = []
            for c in range(cols):
                s_c = jnp.dot(qh, k_ref[c * LANES:(c + 1) * LANES, :], preferred_element_type=jnp.float32)
                if masked:
                    s_c = jnp.where(allowed[c], s_c, NEG)
                s.append(s_c)
            top = s[0]
            for c in range(1, cols):
                top = jnp.maximum(top, s[c])
            m_prev = m_sc[h]
            m_next = jnp.maximum(m_prev, jnp.max(top, axis=1, keepdims=True))
            m_b = m_next[:, 0:1]
            part = None
            pv = None
            for c in range(cols):
                p = jnp.exp((s[c] - m_b) * scale)
                if masked:
                    p = jnp.where(allowed[c], p, 0.0)
                part = p if part is None else part + p
                term = jnp.dot(
                    p.astype(jnp.bfloat16), v_ref[c * LANES:(c + 1) * LANES, :], preferred_element_type=jnp.float32
                )
                pv = term if pv is None else pv + term
            alpha = jnp.exp((m_prev - m_next) * scale)
            l_sc[h] = alpha * l_sc[h] + part
            acc_sc[h] = alpha[:, 0:1] * acc_sc[h] + pv
            m_sc[h] = m_next

    for sub, (k_ref, v_ref) in enumerate(((k0_ref, v0_ref), (k1_ref, v1_ref))):
        shard = me - (steps - 1) + j * per_step + sub
        live = shard >= first
        full = (shard < me) & (shard * shard_rows >= q_last_start)
        pl.when(live & full)(functools.partial(block, False, shard, k_ref, v_ref))
        pl.when(live & jnp.logical_not(full))(functools.partial(block, True, shard, k_ref, v_ref))

    @pl.when(j == grid_steps - 1)
    def _finish():
        for h in range(heads):
            denominator = jnp.sum(l_sc[h], axis=1, keepdims=True)
            o_ref[:, h * HEAD_WIDTH:(h + 1) * HEAD_WIDTH] = (acc_sc[h] / denominator).astype(o_ref.dtype)


def attention(scalars, chunk, queries, kv, q_start, q_pos, after, n_xy, shard_rows):
    rows, width = queries.shape
    heads = width // HEAD_WIDTH
    steps = -(-(MOST - 1) // shard_rows) + 1
    scale = HEAD_WIDTH ** (-0.5)

    at = 4 * chunk

    per_step = 2
    steps = -(-steps // per_step) * per_step

    def index(j, sc, sub, half):
        s = jnp.maximum(sc[at] - (steps - 1) + j * per_step + sub, sc[at + 1])
        slot = jnp.where(s // n_xy == sc[at + 3], 0, 1)
        return (s % n_xy, slot, 0, half)

    groups, _, piece, _ = q_start.shape
    kernel = functools.partial(attn_kernel, steps, per_step, shard_rows, heads, scale, at)
    return pl.pallas_call(
        kernel,
        out_shape=jax.ShapeDtypeStruct((rows, width), jnp.bfloat16),
        grid_spec=pltpu.PrefetchScalarGridSpec(
            num_scalar_prefetch=1,
            grid=(steps // per_step,),
            in_specs=[
                pl.BlockSpec((rows, width), lambda j, sc: (0, 0)),
                pl.BlockSpec((None, None, shard_rows, HEAD_WIDTH), lambda j, sc: index(j, sc, 0, 0)),
                pl.BlockSpec((None, None, shard_rows, HEAD_WIDTH), lambda j, sc: index(j, sc, 0, 1)),
                pl.BlockSpec((None, None, shard_rows, HEAD_WIDTH), lambda j, sc: index(j, sc, 1, 0)),
                pl.BlockSpec((None, None, shard_rows, HEAD_WIDTH), lambda j, sc: index(j, sc, 1, 1)),
                pl.BlockSpec((groups, None, piece, LANES), lambda j, sc: (0, chunk, 0, 0)),
                pl.BlockSpec((groups, None, piece, LANES), lambda j, sc: (0, chunk, 0, 0)),
                pl.BlockSpec(memory_space=pl.ANY),
            ],
            out_specs=pl.BlockSpec((rows, width), lambda j, sc: (0, 0)),
            scratch_shapes=[
                pltpu.VMEM((heads, rows, LANES), jnp.float32),
                pltpu.VMEM((heads, rows, LANES), jnp.float32),
                pltpu.VMEM((heads, rows, HEAD_WIDTH), jnp.float32),
            ],
        ),
        compiler_params=pltpu.CompilerParams(dimension_semantics=("arbitrary",)),
        cost_estimate=pl.CostEstimate(
            flops=4 * steps * heads * rows * shard_rows * HEAD_WIDTH,
            transcendentals=steps * heads * rows * shard_rows,
            bytes_accessed=steps * shard_rows * 2 * HEAD_WIDTH * 2 + 2 * rows * width * 2,
        ),
    )(scalars, queries, kv, kv, kv, kv, q_start, q_pos, after)


def core_step(projected, n_head, piece):
    me_head = lax.axis_index("head")
    held = projected.reshape((n_head // 2, 2, piece) + projected.shape[1:])
    core = me_head % 2
    keep = lax.dynamic_index_in_dim(held, core, axis=1, keepdims=False)
    send = lax.dynamic_index_in_dim(held, 1 - core, axis=1, keepdims=False)
    got = lax.ppermute(send, "head", perm=[(i, i ^ 1) for i in range(n_head)])
    return keep.astype(jnp.float32) + got.astype(jnp.float32)


def chip_step(held, n_head):
    chip = lax.axis_index("head") // 2
    total = lax.dynamic_index_in_dim(held, chip, axis=0, keepdims=False)
    for k in range(1, n_head // 2):
        send = lax.dynamic_index_in_dim(held, chip ^ k, axis=0, keepdims=False)
        got = lax.ppermute(send.astype(jnp.bfloat16), "head", perm=[(i, i ^ (2 * k)) for i in range(n_head)])
        total = total + got.astype(jnp.float32)
    return total.astype(jnp.bfloat16)


def per_device(n_xy, n_head, queries, key_matrix, value_matrix, doc_ids, out_weight):
    rows = queries.shape[0]
    zh = lax.axis_index("zh")
    me = zh * n_xy + lax.axis_index("xy")

    width = key_matrix.shape[1]
    k_t = key_matrix.T.reshape(width, rows // LANES, LANES).transpose(1, 0, 2).reshape(rows, width)
    kv = jnp.concatenate([k_t, value_matrix], axis=1)
    lanes = kv.shape[1]
    tile = 8
    ids = jnp.full((tile * lanes,), -1.0, jnp.float32).at[:rows].set(doc_ids.astype(jnp.float32))
    block = jnp.concatenate([kv, ids.reshape(tile, lanes).astype(kv.dtype)], axis=0)

    partner = lax.ppermute(block, "zh", perm=[(0, 1), (1, 0)])
    pair = jnp.stack([block, partner])
    gathered = lax.all_gather(pair, "xy")

    id_rows = gathered[:, :, rows:, :].astype(jnp.float32)
    docs = jnp.arange(DOCS, dtype=jnp.float32)
    counts = jnp.sum((id_rows[..., None] == docs).astype(jnp.float32), axis=(0, 1, 2, 3))
    below = (jnp.arange(DOCS, dtype=jnp.int32)[None, :] < doc_ids[:, None]).astype(jnp.float32)
    q_start = jnp.sum(below * counts[None, :], axis=1).astype(jnp.int32)
    q_pos = me * rows + jnp.arange(rows, dtype=jnp.int32)

    per_head = rows // n_head
    piece = per_head // CHUNKS

    def chunk_of(x, c):
        x = x.reshape((n_head, CHUNKS, piece) + x.shape[1:])[:, c]
        return x.reshape((n_head * piece,) + x.shape[2:])

    def rows_view(x):
        return jnp.broadcast_to(x[:, None], (rows, LANES)).reshape(n_head, CHUNKS, piece, LANES)

    q_start_b = rows_view(q_start)
    q_pos_b = rows_view(q_pos)
    q_start_c = q_start.reshape(n_head, CHUNKS, piece)
    firsts = jnp.maximum(q_start_c[0, :, 0] // rows, 0)
    lasts = q_start_c[n_head - 1, :, piece - 1]
    scalars = jnp.stack(
        [jnp.full((CHUNKS,), me), firsts, lasts, jnp.full((CHUNKS,), zh)], axis=1
    ).reshape(-1).astype(jnp.int32)

    outs = []
    after = gathered
    for c in range(CHUNKS):
        attended = attention(scalars, c, chunk_of(queries, c), gathered, q_start_b, q_pos_b, after, n_xy, rows)
        projected = jnp.dot(attended, out_weight, preferred_element_type=jnp.float32).astype(jnp.bfloat16)
        after = projected
        if c < CHUNKS - 1:
            outs.append(lax.psum_scatter(projected, "head", scatter_dimension=0, tiled=True))
        else:
            held = core_step(projected, n_head, piece)
            *outs, held = lax.optimization_barrier((*outs, held))
            outs.append(chip_step(held, n_head))
    return jnp.concatenate(outs, axis=0)


def solution(mesh):
    n_ctx = mesh.shape["ctx"]
    n_head = mesh.shape["head"]
    n_zh = 2
    n_xy = n_ctx // n_zh
    devices = np.asarray(mesh.devices).reshape(n_zh, n_xy, n_head)
    inner = Mesh(devices, ("zh", "xy", "head"))
    ctx = ("zh", "xy")
    placed = (P(ctx, "head"), P(ctx, "head"), P(ctx, "head"), P(ctx), P("head", None))
    return jax.shard_map(
        functools.partial(per_device, n_xy, n_head),
        mesh=inner,
        in_specs=placed,
        out_specs=P(("zh", "xy", "head"), None),
        check_vma=False,
    )
```

```python
import functools

import jax
import jax.numpy as jnp
import numpy as np
from jax import lax
from jax.experimental import pallas as pl
from jax.experimental.pallas import tpu as pltpu
from jax.sharding import Mesh, PartitionSpec as P

HEAD_WIDTH = 128
LANES = 128
MOST = 6528
DOCS = 16
NEG = -1e30
CHUNKS = 2
HALVES = 2


def attn_kernel(
    steps, shard_rows, heads, scale, at, sc_ref, q_ref, k_ref, v_ref, qs_ref, qp_ref, after_ref, o_ref, m_sc, l_sc, acc_sc
):
    j = pl.program_id(0)
    me = sc_ref[at]
    first = sc_ref[at + 1]
    q_last_start = sc_ref[at + 2]
    shard = me - (steps - 1) + j
    rows = q_ref.shape[0]

    @pl.when(j == 0)
    def _init():
        m_sc[...] = jnp.full(m_sc.shape, NEG, jnp.float32)
        l_sc[...] = jnp.zeros(l_sc.shape, jnp.float32)
        acc_sc[...] = jnp.zeros(acc_sc.shape, jnp.float32)

    def block(masked):
        cols = shard_rows // LANES
        part_rows = rows // HALVES
        lane = lax.broadcasted_iota(jnp.int32, (part_rows, LANES), 1)
        for half in range(HALVES):
            r = slice(half * part_rows, (half + 1) * part_rows)
            if masked:
                q_start = qs_ref[...].reshape(rows, LANES)[r, 0:1]
                q_pos = qp_ref[...].reshape(rows, LANES)[r, 0:1]
                allowed = []
                for c in range(cols):
                    k_pos = shard * shard_rows + c * LANES + lane
                    allowed.append((k_pos >= q_start) & (k_pos <= q_pos))
            for h in range(heads):
                qh = q_ref[r, h * HEAD_WIDTH:(h + 1) * HEAD_WIDTH]
                s = []
                for c in range(cols):
                    s_c = jnp.dot(qh, k_ref[c * LANES:(c + 1) * LANES, :], preferred_element_type=jnp.float32)
                    if masked:
                        s_c = jnp.where(allowed[c], s_c, NEG)
                    s.append(s_c)
                top = s[0]
                for c in range(1, cols):
                    top = jnp.maximum(top, s[c])
                m_prev = m_sc[h, r, :]
                m_next = jnp.maximum(m_prev, jnp.max(top, axis=1, keepdims=True))
                m_b = m_next[:, 0:1]
                part = None
                pv = None
                for c in range(cols):
                    p = jnp.exp((s[c] - m_b) * scale)
                    if masked:
                        p = jnp.where(allowed[c], p, 0.0)
                    part = p if part is None else part + p
                    term = jnp.dot(
                        p.astype(jnp.bfloat16), v_ref[c * LANES:(c + 1) * LANES, :], preferred_element_type=jnp.float32
                    )
                    pv = term if pv is None else pv + term
                alpha = jnp.exp((m_prev - m_next) * scale)
                l_sc[h, r, :] = alpha * l_sc[h, r, :] + part
                acc_sc[h, r, :] = alpha[:, 0:1] * acc_sc[h, r, :] + pv
                m_sc[h, r, :] = m_next

    live = shard >= first
    full = (shard < me) & (shard * shard_rows >= q_last_start)

    @pl.when(live & full)
    def _full():
        block(False)

    @pl.when(live & jnp.logical_not(full))
    def _masked():
        block(True)

    @pl.when(j == steps - 1)
    def _finish():
        for h in range(heads):
            denominator = jnp.sum(l_sc[h], axis=1, keepdims=True)
            o_ref[:, h * HEAD_WIDTH:(h + 1) * HEAD_WIDTH] = (acc_sc[h] / denominator).astype(o_ref.dtype)


def attention(scalars, chunk, queries, kv, q_start, q_pos, after, n_xy, shard_rows):
    rows, width = queries.shape
    heads = width // HEAD_WIDTH
    steps = -(-(MOST - 1) // shard_rows) + 1
    scale = HEAD_WIDTH ** (-0.5)

    at = 4 * chunk

    def index(j, sc, half):
        s = jnp.maximum(sc[at] - (steps - 1) + j, sc[at + 1])
        slot = jnp.where(s // n_xy == sc[at + 3], 0, 1)
        return (s % n_xy, slot, 0, half)

    groups, _, piece, _ = q_start.shape
    kernel = functools.partial(attn_kernel, steps, shard_rows, heads, scale, at)
    return pl.pallas_call(
        kernel,
        out_shape=jax.ShapeDtypeStruct((rows, width), jnp.bfloat16),
        grid_spec=pltpu.PrefetchScalarGridSpec(
            num_scalar_prefetch=1,
            grid=(steps,),
            in_specs=[
                pl.BlockSpec((rows, width), lambda j, sc: (0, 0)),
                pl.BlockSpec((None, None, shard_rows, HEAD_WIDTH), lambda j, sc: index(j, sc, 0)),
                pl.BlockSpec((None, None, shard_rows, HEAD_WIDTH), lambda j, sc: index(j, sc, 1)),
                pl.BlockSpec((groups, None, piece, LANES), lambda j, sc: (0, chunk, 0, 0)),
                pl.BlockSpec((groups, None, piece, LANES), lambda j, sc: (0, chunk, 0, 0)),
                pl.BlockSpec(memory_space=pl.ANY),
            ],
            out_specs=pl.BlockSpec((rows, width), lambda j, sc: (0, 0)),
            scratch_shapes=[
                pltpu.VMEM((heads, rows, LANES), jnp.float32),
                pltpu.VMEM((heads, rows, LANES), jnp.float32),
                pltpu.VMEM((heads, rows, HEAD_WIDTH), jnp.float32),
            ],
        ),
        compiler_params=pltpu.CompilerParams(dimension_semantics=("arbitrary",)),
        cost_estimate=pl.CostEstimate(
            flops=4 * steps * heads * rows * shard_rows * HEAD_WIDTH,
            transcendentals=steps * heads * rows * shard_rows,
            bytes_accessed=steps * shard_rows * 2 * HEAD_WIDTH * 2 + 2 * rows * width * 2,
        ),
    )(scalars, queries, kv, kv, q_start, q_pos, after)


def core_step(projected, n_head, piece):
    me_head = lax.axis_index("head")
    held = projected.reshape((n_head // 2, 2, piece) + projected.shape[1:])
    core = me_head % 2
    keep = lax.dynamic_index_in_dim(held, core, axis=1, keepdims=False)
    send = lax.dynamic_index_in_dim(held, 1 - core, axis=1, keepdims=False)
    got = lax.ppermute(send, "head", perm=[(i, i ^ 1) for i in range(n_head)])
    return keep.astype(jnp.float32) + got.astype(jnp.float32)


def chip_step(held, n_head):
    chip = lax.axis_index("head") // 2
    total = lax.dynamic_index_in_dim(held, chip, axis=0, keepdims=False)
    for k in range(1, n_head // 2):
        send = lax.dynamic_index_in_dim(held, chip ^ k, axis=0, keepdims=False)
        got = lax.ppermute(send.astype(jnp.bfloat16), "head", perm=[(i, i ^ (2 * k)) for i in range(n_head)])
        total = total + got.astype(jnp.float32)
    return total.astype(jnp.bfloat16)


def per_device(n_xy, n_head, queries, key_matrix, value_matrix, doc_ids, out_weight):
    rows = queries.shape[0]
    zh = lax.axis_index("zh")
    me = zh * n_xy + lax.axis_index("xy")

    width = key_matrix.shape[1]
    k_t = key_matrix.T.reshape(width, rows // LANES, LANES).transpose(1, 0, 2).reshape(rows, width)
    kv = jnp.concatenate([k_t, value_matrix], axis=1)
    lanes = kv.shape[1]
    tile = 8
    ids = jnp.full((tile * lanes,), -1.0, jnp.float32).at[:rows].set(doc_ids.astype(jnp.float32))
    block = jnp.concatenate([kv, ids.reshape(tile, lanes).astype(kv.dtype)], axis=0)

    partner = lax.ppermute(block, "zh", perm=[(0, 1), (1, 0)])
    pair = jnp.stack([block, partner])
    gathered = lax.all_gather(pair, "xy")

    id_rows = gathered[:, :, rows:, :].astype(jnp.float32)
    docs = jnp.arange(DOCS, dtype=jnp.float32)
    counts = jnp.sum((id_rows[..., None] == docs).astype(jnp.float32), axis=(0, 1, 2, 3))
    below = (jnp.arange(DOCS, dtype=jnp.int32)[None, :] < doc_ids[:, None]).astype(jnp.float32)
    q_start = jnp.sum(below * counts[None, :], axis=1).astype(jnp.int32)
    q_pos = me * rows + jnp.arange(rows, dtype=jnp.int32)

    per_head = rows // n_head
    piece = per_head // CHUNKS

    def chunk_of(x, c):
        x = x.reshape((n_head, CHUNKS, piece) + x.shape[1:])[:, c]
        return x.reshape((n_head * piece,) + x.shape[2:])

    def rows_view(x):
        return jnp.broadcast_to(x[:, None], (rows, LANES)).reshape(n_head, CHUNKS, piece, LANES)

    q_start_b = rows_view(q_start)
    q_pos_b = rows_view(q_pos)
    q_start_c = q_start.reshape(n_head, CHUNKS, piece)
    firsts = jnp.maximum(q_start_c[0, :, 0] // rows, 0)
    lasts = q_start_c[n_head - 1, :, piece - 1]
    scalars = jnp.stack(
        [jnp.full((CHUNKS,), me), firsts, lasts, jnp.full((CHUNKS,), zh)], axis=1
    ).reshape(-1).astype(jnp.int32)

    outs = []
    after = gathered
    for c in range(CHUNKS):
        attended = attention(scalars, c, chunk_of(queries, c), gathered, q_start_b, q_pos_b, after, n_xy, rows)
        projected = jnp.dot(attended, out_weight, preferred_element_type=jnp.float32).astype(jnp.bfloat16)
        after = projected
        if c < CHUNKS - 1:
            outs.append(lax.psum_scatter(projected, "head", scatter_dimension=0, tiled=True))
        else:
            held = core_step(projected, n_head, piece)
            *outs, held = lax.optimization_barrier((*outs, held))
            outs.append(chip_step(held, n_head))
    return jnp.concatenate(outs, axis=0)


def solution(mesh):
    n_ctx = mesh.shape["ctx"]
    n_head = mesh.shape["head"]
    n_zh = 2
    n_xy = n_ctx // n_zh
    devices = np.asarray(mesh.devices).reshape(n_zh, n_xy, n_head)
    inner = Mesh(devices, ("zh", "xy", "head"))
    ctx = ("zh", "xy")
    placed = (P(ctx, "head"), P(ctx, "head"), P(ctx, "head"), P(ctx), P("head", None))
    return jax.shard_map(
        functools.partial(per_device, n_xy, n_head),
        mesh=inner,
        in_specs=placed,
        out_specs=P(("zh", "xy", "head"), None),
        check_vma=False,
    )
```

```python
import functools

import jax
import jax.numpy as jnp
import numpy as np
from jax import lax
from jax.experimental import pallas as pl
from jax.experimental.pallas import tpu as pltpu
from jax.sharding import Mesh, PartitionSpec as P

HEAD_WIDTH = 128
LANES = 128
MOST = 6528
DOCS = 16
NEG = -1e30
CHUNKS = 2


def attn_kernel(
    steps, shard_rows, heads, scale, at, sc_ref, q_ref, k_ref, v_ref, qs_ref, qp_ref, after_ref, o_ref, m_sc, l_sc, acc_sc
):
    j = pl.program_id(0)
    me = sc_ref[at]
    first = sc_ref[at + 1]
    q_last_start = sc_ref[at + 2]
    shard = me - (steps - 1) + j
    rows = q_ref.shape[0]

    @pl.when(j == 0)
    def _init():
        m_sc[...] = jnp.full(m_sc.shape, NEG, jnp.float32)
        l_sc[...] = jnp.zeros(l_sc.shape, jnp.float32)
        acc_sc[...] = jnp.zeros(acc_sc.shape, jnp.float32)

    def block(masked):
        cols = shard_rows // LANES
        if masked:
            lane = lax.broadcasted_iota(jnp.int32, (rows, LANES), 1)
            q_start = qs_ref[...].reshape(rows, LANES)[:, 0:1]
            q_pos = qp_ref[...].reshape(rows, LANES)[:, 0:1]
            allowed = []
            for c in range(cols):
                k_pos = shard * shard_rows + c * LANES + lane
                allowed.append((k_pos >= q_start) & (k_pos <= q_pos))
        for h in range(heads):
            qh = q_ref[:, h * HEAD_WIDTH:(h + 1) * HEAD_WIDTH]
            s = []
            for c in range(cols):
                s_c = jnp.dot(qh, k_ref[c * LANES:(c + 1) * LANES, :], preferred_element_type=jnp.float32)
                if masked:
                    s_c = jnp.where(allowed[c], s_c, NEG)
                s.append(s_c)
            top = s[0]
            for c in range(1, cols):
                top = jnp.maximum(top, s[c])
            m_prev = m_sc[h]
            m_next = jnp.maximum(m_prev, jnp.max(top, axis=1, keepdims=True))
            m_b = m_next[:, 0:1]
            part = None
            pv = None
            for c in range(cols):
                p = jnp.exp((s[c] - m_b) * scale)
                if masked:
                    p = jnp.where(allowed[c], p, 0.0)
                part = p if part is None else part + p
                term = jnp.dot(
                    p.astype(jnp.bfloat16), v_ref[c * LANES:(c + 1) * LANES, :], preferred_element_type=jnp.float32
                )
                pv = term if pv is None else pv + term
            alpha = jnp.exp((m_prev - m_next) * scale)
            l_sc[h] = alpha * l_sc[h] + part
            acc_sc[h] = alpha[:, 0:1] * acc_sc[h] + pv
            m_sc[h] = m_next

    live = shard >= first
    full = (shard < me) & (shard * shard_rows >= q_last_start)

    @pl.when(live & full)
    def _full():
        block(False)

    @pl.when(live & jnp.logical_not(full))
    def _masked():
        block(True)

    @pl.when(j == steps - 1)
    def _finish():
        for h in range(heads):
            denominator = jnp.sum(l_sc[h], axis=1, keepdims=True)
            o_ref[:, h * HEAD_WIDTH:(h + 1) * HEAD_WIDTH] = (acc_sc[h] / denominator).astype(o_ref.dtype)


def attention(scalars, chunk, queries, kv, q_start, q_pos, after, n_xy, shard_rows):
    rows, width = queries.shape
    heads = width // HEAD_WIDTH
    steps = -(-(MOST - 1) // shard_rows) + 1
    scale = HEAD_WIDTH ** (-0.5)

    at = 4 * chunk

    def index(j, sc, half):
        s = jnp.maximum(sc[at] - (steps - 1) + j, sc[at + 1])
        slot = jnp.where(s // n_xy == sc[at + 3], 0, 1)
        return (s % n_xy, slot, 0, half)

    groups, _, piece, _ = q_start.shape
    kernel = functools.partial(attn_kernel, steps, shard_rows, heads, scale, at)
    return pl.pallas_call(
        kernel,
        out_shape=jax.ShapeDtypeStruct((rows, width), jnp.bfloat16),
        grid_spec=pltpu.PrefetchScalarGridSpec(
            num_scalar_prefetch=1,
            grid=(steps,),
            in_specs=[
                pl.BlockSpec((rows, width), lambda j, sc: (0, 0)),
                pl.BlockSpec((None, None, shard_rows, HEAD_WIDTH), lambda j, sc: index(j, sc, 0)),
                pl.BlockSpec((None, None, shard_rows, HEAD_WIDTH), lambda j, sc: index(j, sc, 1)),
                pl.BlockSpec((groups, None, piece, LANES), lambda j, sc: (0, chunk, 0, 0)),
                pl.BlockSpec((groups, None, piece, LANES), lambda j, sc: (0, chunk, 0, 0)),
                pl.BlockSpec(memory_space=pl.ANY),
            ],
            out_specs=pl.BlockSpec((rows, width), lambda j, sc: (0, 0)),
            scratch_shapes=[
                pltpu.VMEM((heads, rows, LANES), jnp.float32),
                pltpu.VMEM((heads, rows, LANES), jnp.float32),
                pltpu.VMEM((heads, rows, HEAD_WIDTH), jnp.float32),
            ],
        ),
        compiler_params=pltpu.CompilerParams(dimension_semantics=("arbitrary",)),
        cost_estimate=pl.CostEstimate(
            flops=4 * steps * heads * rows * shard_rows * HEAD_WIDTH,
            transcendentals=steps * heads * rows * shard_rows,
            bytes_accessed=steps * shard_rows * 2 * HEAD_WIDTH * 2 + 2 * rows * width * 2,
        ),
    )(scalars, queries, kv, kv, q_start, q_pos, after)


def core_step(projected, n_head, piece):
    me_head = lax.axis_index("head")
    held = projected.reshape((n_head // 2, 2, piece) + projected.shape[1:])
    core = me_head % 2
    keep = lax.dynamic_index_in_dim(held, core, axis=1, keepdims=False)
    send = lax.dynamic_index_in_dim(held, 1 - core, axis=1, keepdims=False)
    got = lax.ppermute(send, "head", perm=[(i, i ^ 1) for i in range(n_head)])
    return keep.astype(jnp.float32) + got.astype(jnp.float32)


def chip_step(held, n_head):
    chip = lax.axis_index("head") // 2
    total = lax.dynamic_index_in_dim(held, chip, axis=0, keepdims=False)
    for k in range(1, n_head // 2):
        send = lax.dynamic_index_in_dim(held, chip ^ k, axis=0, keepdims=False)
        got = lax.ppermute(send.astype(jnp.bfloat16), "head", perm=[(i, i ^ (2 * k)) for i in range(n_head)])
        total = total + got.astype(jnp.float32)
    return total.astype(jnp.bfloat16)


def per_device(n_xy, n_head, queries, key_matrix, value_matrix, doc_ids, out_weight):
    rows = queries.shape[0]
    zh = lax.axis_index("zh")
    me = zh * n_xy + lax.axis_index("xy")

    width = key_matrix.shape[1]
    k_t = key_matrix.T.reshape(width, rows // LANES, LANES).transpose(1, 0, 2).reshape(rows, width)
    kv = jnp.concatenate([k_t, value_matrix], axis=1)
    lanes = kv.shape[1]
    tile = 8
    ids = jnp.full((tile * lanes,), -1.0, jnp.float32).at[:rows].set(doc_ids.astype(jnp.float32))
    block = jnp.concatenate([kv, ids.reshape(tile, lanes).astype(kv.dtype)], axis=0)

    partner = lax.ppermute(block, "zh", perm=[(0, 1)])
    pair = jnp.stack([block, partner])
    gathered = lax.all_gather(pair, "xy")

    id_rows = gathered[:, :, rows:, :].astype(jnp.float32)
    docs = jnp.arange(DOCS, dtype=jnp.float32)
    slot_used = jnp.stack([jnp.float32(1.0), (zh == 1).astype(jnp.float32)])
    hits = (id_rows[..., None] == docs).astype(jnp.float32) * slot_used[None, :, None, None, None]
    counts = jnp.sum(hits, axis=(0, 1, 2, 3))
    below = (jnp.arange(DOCS, dtype=jnp.int32)[None, :] < doc_ids[:, None]).astype(jnp.float32)
    q_start = jnp.sum(below * counts[None, :], axis=1).astype(jnp.int32)
    q_pos = me * rows + jnp.arange(rows, dtype=jnp.int32)

    per_head = rows // n_head
    piece = per_head // CHUNKS

    def chunk_of(x, c):
        x = x.reshape((n_head, CHUNKS, piece) + x.shape[1:])[:, c]
        return x.reshape((n_head * piece,) + x.shape[2:])

    def rows_view(x):
        return jnp.broadcast_to(x[:, None], (rows, LANES)).reshape(n_head, CHUNKS, piece, LANES)

    q_start_b = rows_view(q_start)
    q_pos_b = rows_view(q_pos)
    q_start_c = q_start.reshape(n_head, CHUNKS, piece)
    firsts = jnp.maximum(q_start_c[0, :, 0] // rows, 0)
    lasts = q_start_c[n_head - 1, :, piece - 1]
    scalars = jnp.stack(
        [jnp.full((CHUNKS,), me), firsts, lasts, jnp.full((CHUNKS,), zh)], axis=1
    ).reshape(-1).astype(jnp.int32)

    outs = []
    after = gathered
    for c in range(CHUNKS):
        attended = attention(scalars, c, chunk_of(queries, c), gathered, q_start_b, q_pos_b, after, n_xy, rows)
        projected = jnp.dot(attended, out_weight, preferred_element_type=jnp.float32).astype(jnp.bfloat16)
        after = projected
        if c < CHUNKS - 1:
            outs.append(lax.psum_scatter(projected, "head", scatter_dimension=0, tiled=True))
        else:
            held = core_step(projected, n_head, piece)
            *outs, held = lax.optimization_barrier((*outs, held))
            outs.append(chip_step(held, n_head))
    return jnp.concatenate(outs, axis=0)


def solution(mesh):
    n_ctx = mesh.shape["ctx"]
    n_head = mesh.shape["head"]
    n_zh = 2
    n_xy = n_ctx // n_zh
    devices = np.asarray(mesh.devices).reshape(n_zh, n_xy, n_head)
    inner = Mesh(devices, ("zh", "xy", "head"))
    ctx = ("zh", "xy")
    placed = (P(ctx, "head"), P(ctx, "head"), P(ctx, "head"), P(ctx), P("head", None))
    return jax.shard_map(
        functools.partial(per_device, n_xy, n_head),
        mesh=inner,
        in_specs=placed,
        out_specs=P(("zh", "xy", "head"), None),
        check_vma=False,
    )
```

```python
import functools

import jax
import jax.numpy as jnp
import numpy as np
from jax import lax
from jax.experimental import pallas as pl
from jax.experimental.pallas import tpu as pltpu
from jax.sharding import Mesh, PartitionSpec as P

HEAD_WIDTH = 128
LANES = 128
MOST = 6528
DOCS = 16
NEG = -1e30
CHUNKS = 2


def attn_kernel(
    steps, shard_rows, heads, scale, at, sc_ref, q_ref, k_ref, v_ref, qs_ref, qp_ref, after_ref, o_ref, m_sc, l_sc, acc_sc
):
    j = pl.program_id(0)
    me = sc_ref[at]
    first = sc_ref[at + 1]
    q_last_start = sc_ref[at + 2]
    shard = me - (steps - 1) + j
    rows = q_ref.shape[0]

    @pl.when(j == 0)
    def _init():
        m_sc[...] = jnp.full(m_sc.shape, NEG, jnp.float32)
        l_sc[...] = jnp.zeros(l_sc.shape, jnp.float32)
        acc_sc[...] = jnp.zeros(acc_sc.shape, jnp.float32)

    def block(masked):
        cols = shard_rows // LANES
        if masked:
            lane = lax.broadcasted_iota(jnp.int32, (rows, LANES), 1)
            q_start = qs_ref[...].reshape(rows, LANES)[:, 0:1]
            q_pos = qp_ref[...].reshape(rows, LANES)[:, 0:1]
            allowed = []
            for c in range(cols):
                k_pos = shard * shard_rows + c * LANES + lane
                allowed.append((k_pos >= q_start) & (k_pos <= q_pos))
        for h in range(heads):
            qh = q_ref[:, h * HEAD_WIDTH:(h + 1) * HEAD_WIDTH]
            s = []
            for c in range(cols):
                s_c = jnp.dot(qh, k_ref[c * LANES:(c + 1) * LANES, :], preferred_element_type=jnp.float32)
                if masked:
                    s_c = jnp.where(allowed[c], s_c, NEG)
                s.append(s_c)
            top = s[0]
            for c in range(1, cols):
                top = jnp.maximum(top, s[c])
            m_prev = m_sc[h]
            m_next = jnp.maximum(m_prev, jnp.max(top, axis=1, keepdims=True))
            m_b = m_next[:, 0:1]
            part = None
            pv = None
            for c in range(cols):
                p = jnp.exp((s[c] - m_b) * scale)
                if masked:
                    p = jnp.where(allowed[c], p, 0.0)
                part = p if part is None else part + p
                term = jnp.dot(
                    p.astype(jnp.bfloat16), v_ref[c * LANES:(c + 1) * LANES, :], preferred_element_type=jnp.float32
                )
                pv = term if pv is None else pv + term
            alpha = jnp.exp((m_prev - m_next) * scale)
            l_sc[h] = alpha * l_sc[h] + part
            acc_sc[h] = alpha[:, 0:1] * acc_sc[h] + pv
            m_sc[h] = m_next

    live = shard >= first
    full = (shard < me) & (shard * shard_rows >= q_last_start)

    @pl.when(live & full)
    def _full():
        block(False)

    @pl.when(live & jnp.logical_not(full))
    def _masked():
        block(True)

    @pl.when(j == steps - 1)
    def _finish():
        for h in range(heads):
            denominator = jnp.sum(l_sc[h], axis=1, keepdims=True)
            o_ref[:, h * HEAD_WIDTH:(h + 1) * HEAD_WIDTH] = (acc_sc[h] / denominator).astype(o_ref.dtype)


def attention(scalars, chunk, queries, kv, q_start, q_pos, after, n_xy, shard_rows):
    rows, width = queries.shape
    heads = width // HEAD_WIDTH
    steps = -(-(MOST - 1) // shard_rows) + 1
    scale = HEAD_WIDTH ** (-0.5)

    at = 4 * chunk

    def index(j, sc, half):
        s = jnp.maximum(sc[at] - (steps - 1) + j, sc[at + 1])
        slot = jnp.where(s // n_xy == sc[at + 3], 0, 1)
        return (s % n_xy, slot, 0, half)

    groups, _, piece, _ = q_start.shape
    kernel = functools.partial(attn_kernel, steps, shard_rows, heads, scale, at)
    return pl.pallas_call(
        kernel,
        out_shape=jax.ShapeDtypeStruct((rows, width), jnp.bfloat16),
        grid_spec=pltpu.PrefetchScalarGridSpec(
            num_scalar_prefetch=1,
            grid=(steps,),
            in_specs=[
                pl.BlockSpec((rows, width), lambda j, sc: (0, 0)),
                pl.BlockSpec((None, None, shard_rows, HEAD_WIDTH), lambda j, sc: index(j, sc, 0)),
                pl.BlockSpec((None, None, shard_rows, HEAD_WIDTH), lambda j, sc: index(j, sc, 1)),
                pl.BlockSpec((groups, None, piece, LANES), lambda j, sc: (0, chunk, 0, 0)),
                pl.BlockSpec((groups, None, piece, LANES), lambda j, sc: (0, chunk, 0, 0)),
                pl.BlockSpec(memory_space=pl.ANY),
            ],
            out_specs=pl.BlockSpec((rows, width), lambda j, sc: (0, 0)),
            scratch_shapes=[
                pltpu.VMEM((heads, rows, LANES), jnp.float32),
                pltpu.VMEM((heads, rows, LANES), jnp.float32),
                pltpu.VMEM((heads, rows, HEAD_WIDTH), jnp.float32),
            ],
        ),
        compiler_params=pltpu.CompilerParams(dimension_semantics=("arbitrary",)),
        cost_estimate=pl.CostEstimate(
            flops=4 * steps * heads * rows * shard_rows * HEAD_WIDTH,
            transcendentals=steps * heads * rows * shard_rows,
            bytes_accessed=steps * shard_rows * 2 * HEAD_WIDTH * 2 + 2 * rows * width * 2,
        ),
    )(scalars, queries, kv, kv, q_start, q_pos, after)


def core_step(projected, n_head, piece):
    me_head = lax.axis_index("head")
    held = projected.reshape((n_head // 2, 2, piece) + projected.shape[1:])
    core = me_head % 2
    keep = lax.dynamic_index_in_dim(held, core, axis=1, keepdims=False)
    send = lax.dynamic_index_in_dim(held, 1 - core, axis=1, keepdims=False)
    got = lax.ppermute(send, "head", perm=[(i, i ^ 1) for i in range(n_head)])
    return keep.astype(jnp.float32) + got.astype(jnp.float32)


def chip_step(held, n_head):
    chip = lax.axis_index("head") // 2
    bit = 1
    while bit < n_head // 2:
        mine = (chip // bit) % 2
        held = held.reshape((-1, 2) + held.shape[1:])
        keep = lax.dynamic_index_in_dim(held, mine, axis=1, keepdims=False)
        send = lax.dynamic_index_in_dim(held, 1 - mine, axis=1, keepdims=False)
        got = lax.ppermute(send.astype(jnp.bfloat16), "head", perm=[(i, i ^ (2 * bit)) for i in range(n_head)])
        held = keep + got.astype(jnp.float32)
        bit *= 2
    return held[0].astype(jnp.bfloat16)


def per_device(n_xy, n_head, queries, key_matrix, value_matrix, doc_ids, out_weight):
    rows = queries.shape[0]
    zh = lax.axis_index("zh")
    me = zh * n_xy + lax.axis_index("xy")

    width = key_matrix.shape[1]
    k_t = key_matrix.T.reshape(width, rows // LANES, LANES).transpose(1, 0, 2).reshape(rows, width)
    kv = jnp.concatenate([k_t, value_matrix], axis=1)
    lanes = kv.shape[1]
    tile = 8
    ids = jnp.full((tile * lanes,), -1.0, jnp.float32).at[:rows].set(doc_ids.astype(jnp.float32))
    block = jnp.concatenate([kv, ids.reshape(tile, lanes).astype(kv.dtype)], axis=0)

    partner = lax.ppermute(block, "zh", perm=[(0, 1), (1, 0)])
    pair = jnp.stack([block, partner])
    gathered = lax.all_gather(pair, "xy")

    id_rows = gathered[:, :, rows:, :].astype(jnp.float32)
    docs = jnp.arange(DOCS, dtype=jnp.float32)
    counts = jnp.sum((id_rows[..., None] == docs).astype(jnp.float32), axis=(0, 1, 2, 3))
    below = (jnp.arange(DOCS, dtype=jnp.int32)[None, :] < doc_ids[:, None]).astype(jnp.float32)
    q_start = jnp.sum(below * counts[None, :], axis=1).astype(jnp.int32)
    q_pos = me * rows + jnp.arange(rows, dtype=jnp.int32)

    per_head = rows // n_head
    piece = per_head // CHUNKS

    def chunk_of(x, c):
        x = x.reshape((n_head, CHUNKS, piece) + x.shape[1:])[:, c]
        return x.reshape((n_head * piece,) + x.shape[2:])

    def rows_view(x):
        return jnp.broadcast_to(x[:, None], (rows, LANES)).reshape(n_head, CHUNKS, piece, LANES)

    q_start_b = rows_view(q_start)
    q_pos_b = rows_view(q_pos)
    q_start_c = q_start.reshape(n_head, CHUNKS, piece)
    firsts = jnp.maximum(q_start_c[0, :, 0] // rows, 0)
    lasts = q_start_c[n_head - 1, :, piece - 1]
    scalars = jnp.stack(
        [jnp.full((CHUNKS,), me), firsts, lasts, jnp.full((CHUNKS,), zh)], axis=1
    ).reshape(-1).astype(jnp.int32)

    outs = []
    after = gathered
    for c in range(CHUNKS):
        attended = attention(scalars, c, chunk_of(queries, c), gathered, q_start_b, q_pos_b, after, n_xy, rows)
        projected = jnp.dot(attended, out_weight, preferred_element_type=jnp.float32).astype(jnp.bfloat16)
        after = projected
        if c < CHUNKS - 1:
            outs.append(lax.psum_scatter(projected, "head", scatter_dimension=0, tiled=True))
        else:
            held = core_step(projected, n_head, piece)
            *outs, held = lax.optimization_barrier((*outs, held))
            outs.append(chip_step(held, n_head))
    return jnp.concatenate(outs, axis=0)


def solution(mesh):
    n_ctx = mesh.shape["ctx"]
    n_head = mesh.shape["head"]
    n_zh = 2
    n_xy = n_ctx // n_zh
    devices = np.asarray(mesh.devices).reshape(n_zh, n_xy, n_head)
    inner = Mesh(devices, ("zh", "xy", "head"))
    ctx = ("zh", "xy")
    placed = (P(ctx, "head"), P(ctx, "head"), P(ctx, "head"), P(ctx), P("head", None))
    return jax.shard_map(
        functools.partial(per_device, n_xy, n_head),
        mesh=inner,
        in_specs=placed,
        out_specs=P(("zh", "xy", "head"), None),
        check_vma=False,
    )
```

```python
import functools

import jax
import jax.numpy as jnp
import numpy as np
from jax import lax
from jax.experimental import pallas as pl
from jax.experimental.pallas import tpu as pltpu
from jax.sharding import Mesh, PartitionSpec as P

HEAD_WIDTH = 128
LANES = 128
MOST = 6528
DOCS = 16
NEG = -1e30
CHUNKS = 2


def attn_kernel(
    steps, shard_rows, heads, scale, at, chunk, sc_ref, q_ref, k_ref, v_ref, qs_ref, after_ref, o_ref, m_sc, l_sc, acc_sc
):
    j = pl.program_id(0)
    me = sc_ref[at]
    first = sc_ref[at + 1]
    q_last_start = sc_ref[at + 2]
    shard = me - (steps - 1) + j
    rows = q_ref.shape[0]

    @pl.when(j == 0)
    def _init():
        m_sc[...] = jnp.full(m_sc.shape, NEG, jnp.float32)
        l_sc[...] = jnp.zeros(l_sc.shape, jnp.float32)
        acc_sc[...] = jnp.zeros(acc_sc.shape, jnp.float32)

    def block(masked):
        cols = shard_rows // LANES
        if masked:
            lane = lax.broadcasted_iota(jnp.int32, (rows, LANES), 1)
            q_start = qs_ref[...].reshape(rows, LANES)[:, 0:1]
            groups, piece, _ = qs_ref.shape
            shape = (groups, piece, LANES)
            group = lax.broadcasted_iota(jnp.int32, shape, 0)
            in_piece = lax.broadcasted_iota(jnp.int32, shape, 1)
            q_pos = me * shard_rows + group * (shard_rows // groups) + chunk * piece + in_piece
            q_pos = q_pos.reshape(rows, LANES)[:, 0:1]
            allowed = []
            for c in range(cols):
                k_pos = shard * shard_rows + c * LANES + lane
                allowed.append((k_pos >= q_start) & (k_pos <= q_pos))
        for h in range(heads):
            qh = q_ref[:, h * HEAD_WIDTH:(h + 1) * HEAD_WIDTH]
            s = []
            for c in range(cols):
                s_c = jnp.dot(qh, k_ref[c * LANES:(c + 1) * LANES, :], preferred_element_type=jnp.float32)
                if masked:
                    s_c = jnp.where(allowed[c], s_c, NEG)
                s.append(s_c)
            top = s[0]
            for c in range(1, cols):
                top = jnp.maximum(top, s[c])
            m_prev = m_sc[h]
            m_next = jnp.maximum(m_prev, jnp.max(top, axis=1, keepdims=True))
            m_b = m_next[:, 0:1]
            part = None
            pv = None
            for c in range(cols):
                p = jnp.exp((s[c] - m_b) * scale)
                if masked:
                    p = jnp.where(allowed[c], p, 0.0)
                part = p if part is None else part + p
                term = jnp.dot(
                    p.astype(jnp.bfloat16), v_ref[c * LANES:(c + 1) * LANES, :], preferred_element_type=jnp.float32
                )
                pv = term if pv is None else pv + term
            alpha = jnp.exp((m_prev - m_next) * scale)
            l_sc[h] = alpha * l_sc[h] + part
            acc_sc[h] = alpha[:, 0:1] * acc_sc[h] + pv
            m_sc[h] = m_next

    live = shard >= first
    full = (shard < me) & (shard * shard_rows >= q_last_start)

    @pl.when(live & full)
    def _full():
        block(False)

    @pl.when(live & jnp.logical_not(full))
    def _masked():
        block(True)

    @pl.when(j == steps - 1)
    def _finish():
        for h in range(heads):
            denominator = jnp.sum(l_sc[h], axis=1, keepdims=True)
            o_ref[:, h * HEAD_WIDTH:(h + 1) * HEAD_WIDTH] = (acc_sc[h] / denominator).astype(o_ref.dtype)


def attention(scalars, chunk, queries, kv, q_start, after, n_xy, shard_rows):
    rows, width = queries.shape
    heads = width // HEAD_WIDTH
    steps = -(-(MOST - 1) // shard_rows) + 1
    scale = HEAD_WIDTH ** (-0.5)

    at = 4 * chunk

    def index(j, sc, half):
        s = jnp.maximum(sc[at] - (steps - 1) + j, sc[at + 1])
        slot = jnp.where(s // n_xy == sc[at + 3], 0, 1)
        return (s % n_xy, slot, 0, half)

    groups, _, piece, _ = q_start.shape
    kernel = functools.partial(attn_kernel, steps, shard_rows, heads, scale, at, chunk)
    return pl.pallas_call(
        kernel,
        out_shape=jax.ShapeDtypeStruct((rows, width), jnp.bfloat16),
        grid_spec=pltpu.PrefetchScalarGridSpec(
            num_scalar_prefetch=1,
            grid=(steps,),
            in_specs=[
                pl.BlockSpec((rows, width), lambda j, sc: (0, 0)),
                pl.BlockSpec((None, None, shard_rows, HEAD_WIDTH), lambda j, sc: index(j, sc, 0)),
                pl.BlockSpec((None, None, shard_rows, HEAD_WIDTH), lambda j, sc: index(j, sc, 1)),
                pl.BlockSpec((groups, None, piece, LANES), lambda j, sc: (0, chunk, 0, 0)),
                pl.BlockSpec(memory_space=pl.ANY),
            ],
            out_specs=pl.BlockSpec((rows, width), lambda j, sc: (0, 0)),
            scratch_shapes=[
                pltpu.VMEM((heads, rows, LANES), jnp.float32),
                pltpu.VMEM((heads, rows, LANES), jnp.float32),
                pltpu.VMEM((heads, rows, HEAD_WIDTH), jnp.float32),
            ],
        ),
        compiler_params=pltpu.CompilerParams(dimension_semantics=("arbitrary",)),
        cost_estimate=pl.CostEstimate(
            flops=4 * steps * heads * rows * shard_rows * HEAD_WIDTH,
            transcendentals=steps * heads * rows * shard_rows,
            bytes_accessed=steps * shard_rows * 2 * HEAD_WIDTH * 2 + 2 * rows * width * 2,
        ),
    )(scalars, queries, kv, kv, q_start, after)


def core_step(projected, n_head, piece):
    me_head = lax.axis_index("head")
    held = projected.reshape((n_head // 2, 2, piece) + projected.shape[1:])
    core = me_head % 2
    keep = lax.dynamic_index_in_dim(held, core, axis=1, keepdims=False)
    send = lax.dynamic_index_in_dim(held, 1 - core, axis=1, keepdims=False)
    got = lax.ppermute(send, "head", perm=[(i, i ^ 1) for i in range(n_head)])
    return keep.astype(jnp.float32) + got.astype(jnp.float32)


def chip_step(held, n_head):
    chip = lax.axis_index("head") // 2
    total = lax.dynamic_index_in_dim(held, chip, axis=0, keepdims=False)
    for k in range(1, n_head // 2):
        send = lax.dynamic_index_in_dim(held, chip ^ k, axis=0, keepdims=False)
        got = lax.ppermute(send.astype(jnp.bfloat16), "head", perm=[(i, i ^ (2 * k)) for i in range(n_head)])
        total = total + got.astype(jnp.float32)
    return total.astype(jnp.bfloat16)


def per_device(n_xy, n_head, queries, key_matrix, value_matrix, doc_ids, out_weight):
    rows = queries.shape[0]
    zh = lax.axis_index("zh")
    me = zh * n_xy + lax.axis_index("xy")

    width = key_matrix.shape[1]
    k_t = key_matrix.T.reshape(width, rows // LANES, LANES).transpose(1, 0, 2).reshape(rows, width)
    kv = jnp.concatenate([k_t, value_matrix], axis=1)
    lanes = kv.shape[1]
    tile = 8
    ids = jnp.full((tile * lanes,), -1.0, jnp.float32).at[:rows].set(doc_ids.astype(jnp.float32))
    block = jnp.concatenate([kv, ids.reshape(tile, lanes).astype(kv.dtype)], axis=0)

    partner = lax.ppermute(block, "zh", perm=[(0, 1), (1, 0)])
    pair = jnp.stack([block, partner])
    gathered = lax.all_gather(pair, "xy")

    id_rows = gathered[:, :, rows:, :].astype(jnp.float32)
    docs = jnp.arange(DOCS, dtype=jnp.float32)
    counts = jnp.sum((id_rows[..., None] == docs).astype(jnp.float32), axis=(0, 1, 2, 3))
    below = (jnp.arange(DOCS, dtype=jnp.int32)[None, :] < doc_ids[:, None]).astype(jnp.float32)
    q_start = jnp.sum(below * counts[None, :], axis=1).astype(jnp.int32)
    q_pos = me * rows + jnp.arange(rows, dtype=jnp.int32)

    per_head = rows // n_head
    piece = per_head // CHUNKS

    def chunk_of(x, c):
        x = x.reshape((n_head, CHUNKS, piece) + x.shape[1:])[:, c]
        return x.reshape((n_head * piece,) + x.shape[2:])

    def rows_view(x):
        return jnp.broadcast_to(x[:, None], (rows, LANES)).reshape(n_head, CHUNKS, piece, LANES)

    q_start_b = rows_view(q_start)
    q_start_c = q_start.reshape(n_head, CHUNKS, piece)
    firsts = jnp.maximum(q_start_c[0, :, 0] // rows, 0)
    lasts = q_start_c[n_head - 1, :, piece - 1]
    scalars = jnp.stack(
        [jnp.full((CHUNKS,), me), firsts, lasts, jnp.full((CHUNKS,), zh)], axis=1
    ).reshape(-1).astype(jnp.int32)

    outs = []
    after = gathered
    for c in range(CHUNKS):
        attended = attention(scalars, c, chunk_of(queries, c), gathered, q_start_b, after, n_xy, rows)
        projected = jnp.dot(attended, out_weight, preferred_element_type=jnp.float32).astype(jnp.bfloat16)
        after = projected
        if c < CHUNKS - 1:
            outs.append(lax.psum_scatter(projected, "head", scatter_dimension=0, tiled=True))
        else:
            held = core_step(projected, n_head, piece)
            *outs, held = lax.optimization_barrier((*outs, held))
            outs.append(chip_step(held, n_head))
    return jnp.concatenate(outs, axis=0)


def solution(mesh):
    n_ctx = mesh.shape["ctx"]
    n_head = mesh.shape["head"]
    n_zh = 2
    n_xy = n_ctx // n_zh
    devices = np.asarray(mesh.devices).reshape(n_zh, n_xy, n_head)
    inner = Mesh(devices, ("zh", "xy", "head"))
    ctx = ("zh", "xy")
    placed = (P(ctx, "head"), P(ctx, "head"), P(ctx, "head"), P(ctx), P("head", None))
    return jax.shard_map(
        functools.partial(per_device, n_xy, n_head),
        mesh=inner,
        in_specs=placed,
        out_specs=P(("zh", "xy", "head"), None),
        check_vma=False,
    )
```

```python
import functools

import jax
import jax.numpy as jnp
import numpy as np
from jax import lax
from jax.experimental import pallas as pl
from jax.experimental.pallas import tpu as pltpu
from jax.sharding import Mesh, PartitionSpec as P

HEAD_WIDTH = 128
LANES = 128
MOST = 6528
DOCS = 16
NEG = -1e30
CHUNKS = 2


def attn_kernel(
    steps, shard_rows, heads, scale, at, sc_ref, q_ref, k_ref, v_ref, qs_ref, qp_ref, after_ref, o_ref, m_sc, l_sc, acc_sc
):
    j = pl.program_id(0)
    me = sc_ref[at]
    first = sc_ref[at + 1]
    q_last_start = sc_ref[at + 2]
    shard = me - (steps - 1) + j
    rows = q_ref.shape[0]

    @pl.when(j == 0)
    def _init():
        m_sc[...] = jnp.full(m_sc.shape, NEG, jnp.float32)
        l_sc[...] = jnp.zeros(l_sc.shape, jnp.float32)
        acc_sc[...] = jnp.zeros(acc_sc.shape, jnp.float32)

    def block(masked):
        cols = shard_rows // LANES
        if masked:
            lane = lax.broadcasted_iota(jnp.int32, (rows, LANES), 1)
            q_start = qs_ref[...].reshape(rows, LANES)[:, 0:1]
            q_pos = qp_ref[...].reshape(rows, LANES)[:, 0:1]
            allowed = []
            for c in range(cols):
                k_pos = shard * shard_rows + c * LANES + lane
                allowed.append((k_pos >= q_start) & (k_pos <= q_pos))
        for h in range(heads):
            qh = q_ref[:, h * HEAD_WIDTH:(h + 1) * HEAD_WIDTH]
            s = []
            for c in range(cols):
                s_c = jnp.dot(qh, k_ref[c * LANES:(c + 1) * LANES, :], preferred_element_type=jnp.float32)
                if masked:
                    s_c = jnp.where(allowed[c], s_c, NEG)
                s.append(s_c)
            top = s[0]
            for c in range(1, cols):
                top = jnp.maximum(top, s[c])
            m_prev = m_sc[h]
            m_next = jnp.maximum(m_prev, jnp.max(top, axis=1, keepdims=True))
            m_b = m_next[:, 0:1]
            part = None
            pv = None
            for c in range(cols):
                p = jnp.exp((s[c] - m_b) * scale)
                if masked:
                    p = jnp.where(allowed[c], p, 0.0)
                part = p if part is None else part + p
                term = jnp.dot(
                    p.astype(jnp.bfloat16), v_ref[c * LANES:(c + 1) * LANES, :], preferred_element_type=jnp.float32
                )
                pv = term if pv is None else pv + term
            alpha = jnp.exp((m_prev - m_next) * scale)
            l_sc[h] = alpha * l_sc[h] + part
            acc_sc[h] = alpha[:, 0:1] * acc_sc[h] + pv
            m_sc[h] = m_next

    live = shard >= first
    full = (shard < me) & (shard * shard_rows >= q_last_start)

    @pl.when(live & full)
    def _full():
        block(False)

    @pl.when(live & jnp.logical_not(full))
    def _masked():
        block(True)

    @pl.when(j == steps - 1)
    def _finish():
        for h in range(heads):
            denominator = jnp.sum(l_sc[h], axis=1, keepdims=True)
            o_ref[:, h * HEAD_WIDTH:(h + 1) * HEAD_WIDTH] = (acc_sc[h] / denominator).astype(o_ref.dtype)


def attention(scalars, chunk, queries, kv, q_start, q_pos, after, n_xy, shard_rows):
    rows, width = queries.shape
    heads = width // HEAD_WIDTH
    steps = -(-(MOST - 1) // shard_rows) + 1
    scale = HEAD_WIDTH ** (-0.5)

    at = 4 * chunk

    def index(j, sc, half):
        s = jnp.maximum(sc[at] - (steps - 1) + j, sc[at + 1])
        slot = jnp.where(s // n_xy == sc[at + 3], 0, 1)
        return (s % n_xy, slot, 0, half)

    groups, _, piece, _ = q_start.shape
    kernel = functools.partial(attn_kernel, steps, shard_rows, heads, scale, at)
    return pl.pallas_call(
        kernel,
        out_shape=jax.ShapeDtypeStruct((rows, width), jnp.bfloat16),
        grid_spec=pltpu.PrefetchScalarGridSpec(
            num_scalar_prefetch=1,
            grid=(steps,),
            in_specs=[
                pl.BlockSpec((rows, width), lambda j, sc: (0, 0)),
                pl.BlockSpec((None, None, shard_rows, HEAD_WIDTH), lambda j, sc: index(j, sc, 0)),
                pl.BlockSpec((None, None, shard_rows, HEAD_WIDTH), lambda j, sc: index(j, sc, 1)),
                pl.BlockSpec((groups, None, piece, LANES), lambda j, sc: (0, chunk, 0, 0)),
                pl.BlockSpec((groups, None, piece, LANES), lambda j, sc: (0, chunk, 0, 0)),
                pl.BlockSpec(memory_space=pl.ANY),
            ],
            out_specs=pl.BlockSpec((rows, width), lambda j, sc: (0, 0)),
            scratch_shapes=[
                pltpu.VMEM((heads, rows, LANES), jnp.float32),
                pltpu.VMEM((heads, rows, LANES), jnp.float32),
                pltpu.VMEM((heads, rows, HEAD_WIDTH), jnp.float32),
            ],
        ),
        compiler_params=pltpu.CompilerParams(dimension_semantics=("arbitrary",)),
        cost_estimate=pl.CostEstimate(
            flops=4 * steps * heads * rows * shard_rows * HEAD_WIDTH,
            transcendentals=steps * heads * rows * shard_rows,
            bytes_accessed=steps * shard_rows * 2 * HEAD_WIDTH * 2 + 2 * rows * width * 2,
        ),
    )(scalars, queries, kv, kv, q_start, q_pos, after)


def core_step(projected, n_head, piece):
    me_head = lax.axis_index("head")
    held = projected.reshape((n_head // 2, 2, piece) + projected.shape[1:])
    core = me_head % 2
    keep = lax.dynamic_index_in_dim(held, core, axis=1, keepdims=False)
    send = lax.dynamic_index_in_dim(held, 1 - core, axis=1, keepdims=False)
    got = lax.ppermute(send, "head", perm=[(i, i ^ 1) for i in range(n_head)])
    summed = keep.astype(jnp.float32) + got.astype(jnp.float32)
    return summed, summed.astype(jnp.bfloat16)


def chip_step(held, sent, n_head):
    chip = lax.axis_index("head") // 2
    total = lax.dynamic_index_in_dim(held, chip, axis=0, keepdims=False)
    for k in range(1, n_head // 2):
        send = lax.dynamic_index_in_dim(sent, chip ^ k, axis=0, keepdims=False)
        got = lax.ppermute(send, "head", perm=[(i, i ^ (2 * k)) for i in range(n_head)])
        total = total + got.astype(jnp.float32)
    return total.astype(jnp.bfloat16)


def per_device(n_xy, n_head, queries, key_matrix, value_matrix, doc_ids, out_weight):
    rows = queries.shape[0]
    zh = lax.axis_index("zh")
    me = zh * n_xy + lax.axis_index("xy")

    width = key_matrix.shape[1]
    k_t = key_matrix.T.reshape(width, rows // LANES, LANES).transpose(1, 0, 2).reshape(rows, width)
    kv = jnp.concatenate([k_t, value_matrix], axis=1)
    lanes = kv.shape[1]
    tile = 8
    ids = jnp.full((tile * lanes,), -1.0, jnp.float32).at[:rows].set(doc_ids.astype(jnp.float32))
    block = jnp.concatenate([kv, ids.reshape(tile, lanes).astype(kv.dtype)], axis=0)

    partner = lax.ppermute(block, "zh", perm=[(0, 1), (1, 0)])
    pair = jnp.stack([block, partner])
    gathered = lax.all_gather(pair, "xy")

    id_rows = gathered[:, :, rows:, :].astype(jnp.float32)
    docs = jnp.arange(DOCS, dtype=jnp.float32)
    counts = jnp.sum((id_rows[..., None] == docs).astype(jnp.float32), axis=(0, 1, 2, 3))
    below = (jnp.arange(DOCS, dtype=jnp.int32)[None, :] < doc_ids[:, None]).astype(jnp.float32)
    q_start = jnp.sum(below * counts[None, :], axis=1).astype(jnp.int32)
    q_pos = me * rows + jnp.arange(rows, dtype=jnp.int32)

    per_head = rows // n_head
    piece = per_head // CHUNKS

    def chunk_of(x, c):
        x = x.reshape((n_head, CHUNKS, piece) + x.shape[1:])[:, c]
        return x.reshape((n_head * piece,) + x.shape[2:])

    def rows_view(x):
        return jnp.broadcast_to(x[:, None], (rows, LANES)).reshape(n_head, CHUNKS, piece, LANES)

    q_start_b = rows_view(q_start)
    q_pos_b = rows_view(q_pos)
    q_start_c = q_start.reshape(n_head, CHUNKS, piece)
    firsts = jnp.maximum(q_start_c[0, :, 0] // rows, 0)
    lasts = q_start_c[n_head - 1, :, piece - 1]
    scalars = jnp.stack(
        [jnp.full((CHUNKS,), me), firsts, lasts, jnp.full((CHUNKS,), zh)], axis=1
    ).reshape(-1).astype(jnp.int32)

    outs = []
    after = gathered
    for c in range(CHUNKS):
        attended = attention(scalars, c, chunk_of(queries, c), gathered, q_start_b, q_pos_b, after, n_xy, rows)
        projected = jnp.dot(attended, out_weight, preferred_element_type=jnp.float32).astype(jnp.bfloat16)
        after = projected
        if c < CHUNKS - 1:
            outs.append(lax.psum_scatter(projected, "head", scatter_dimension=0, tiled=True))
        else:
            held, sent = core_step(projected, n_head, piece)
            *outs, held, sent = lax.optimization_barrier((*outs, held, sent))
            outs.append(chip_step(held, sent, n_head))
    return jnp.concatenate(outs, axis=0)


def solution(mesh):
    n_ctx = mesh.shape["ctx"]
    n_head = mesh.shape["head"]
    n_zh = 2
    n_xy = n_ctx // n_zh
    devices = np.asarray(mesh.devices).reshape(n_zh, n_xy, n_head)
    inner = Mesh(devices, ("zh", "xy", "head"))
    ctx = ("zh", "xy")
    placed = (P(ctx, "head"), P(ctx, "head"), P(ctx, "head"), P(ctx), P("head", None))
    return jax.shard_map(
        functools.partial(per_device, n_xy, n_head),
        mesh=inner,
        in_specs=placed,
        out_specs=P(("zh", "xy", "head"), None),
        check_vma=False,
    )
```
